256 devices in a mesh: pipe: 4 (over x_hi, core), ctx: 64 (over x_lo, z, y).
Axes of the slice: x: 4 (x_hi: 2, x_lo: 2; x = x_hi * 2 + x_lo), y: 4, z: 8, core: 2. Of those that a mesh axis runs over, the one named last changes fastest.
Arguments:
- hidden: bfloat16 [2, 8192, 2048], P(None, 'ctx'), may hold values from -6 to 6
- gain: float32 [4, 2048], P('pipe'), may hold values from 0.1 to 1.9
- keys: bfloat16 [4, 2, 8192, 512], P('pipe', None, 'ctx'), may hold values from -4 to 4
- values: bfloat16 [4, 2, 8192, 512], P('pipe', None, 'ctx'), may hold values from -6 to 6
- cotangent: float32 [2, 64, 2048], replicated, may hold values from -384 to 384
- lengths: int32 [2, 64], replicated, may hold values from 1 to 256, as said below
- doc_start: int32 [2, 8192], P(None, 'ctx'), may hold values from 0 to 8191, as said below
- block_mask: int32 [2, 64, 64], replicated, may hold values from 0 to 1, as said below
Outputs:
- grad_stream: bfloat16 [4, 2, 8192, 2048], P('pipe', None, 'ctx')
- grad_keys: bfloat16 [4, 2, 8192, 512], P('pipe', None, 'ctx')
- grad_values: bfloat16 [4, 2, 8192, 512], P('pipe', None, 'ctx')
- grad_gain: float32 [4, 2048], P('pipe')
The draws below stay inside these ranges and needn't reach their ends.
Inputs may be any that keep to these rules, and one draw needn't show every extreme that they name: In each micro-batch the lengths sum to 8192, and one of them is exactly 256. doc_start[m, i] is the first position of the document that holds position i, the documents of lengths[m] lying end to end in order. block_mask[m, a, b] is 1 exactly where some token of block a has an earlier or equal token of its own document in block b, blocks of 128 tokens; else 0.
All inputs are finite; a program needn't handle non-finite values.
Results may differ from the reference program's by a relative error of at most 0.0091.
Values may be sent and summed in bfloat16 or wider, within the bound.
No kernel may reach another device: no remote copies, remote signals or barrier semaphores. Data moves between devices by JAX's collectives and lax.ppermute only.
A program may use at most 128 MiB of HBM per device.

```python
import jax
import jax.numpy as jnp
from jax import lax

HEADS = 16
KV_HEADS = 4
HEAD_DIM = 128
TOK_DEV = 128
MICRO = 2
SECTIONS = 4
SPAN = 2
WIDTH = 2048
KV_WIDTH = 512
TOKENS = 8192
BLOCKS = 64
MAXDOC = 256
DOCS = 64


def document_plan(key):
    remainder = TOKENS - MAXDOC
    others = DOCS - 1
    base_len = remainder // others
    spare = remainder - base_len * others
    move_reach = base_len // 4

    def one_batch(batch_key):
        first_key, second_key = jax.random.split(batch_key)
        starting = base_len + (jnp.arange(others) < spare).astype(jnp.int32)
        transfer = jax.random.randint(first_key, (others,), -move_reach, move_reach + 1).astype(jnp.int32)
        middle = starting - transfer + jnp.roll(transfer, 1)
        doc_lengths = jnp.concatenate([jnp.full((1,), MAXDOC, jnp.int32), middle.astype(jnp.int32)])
        turn = jax.random.randint(second_key, (), 0, DOCS)
        doc_lengths = jnp.roll(doc_lengths, turn)
        doc_ends = jnp.cumsum(doc_lengths)
        starts = doc_ends - doc_lengths
        positions = jnp.arange(TOKENS, dtype=jnp.int32)
        doc_owner = jnp.sum((positions[:, None] >= doc_ends[None, :]).astype(jnp.int32), axis=1)
        first_pos = starts[doc_owner].astype(jnp.int32)
        block_first = first_pos[::TOK_DEV]
        block_ids = jnp.arange(BLOCKS, dtype=jnp.int32)
        allowed = (block_ids[None, :] <= block_ids[:, None]) & ((block_ids[None, :] + 1) * TOK_DEV - 1 >= block_first[:, None])
        return (doc_lengths.astype(jnp.int32), first_pos, allowed.astype(jnp.int32))
    batch_keys = jax.random.split(jax.random.fold_in(key, 4242), MICRO)
    return jax.vmap(one_batch)(batch_keys)


def draw_lengths(key, part):
    return document_plan(key)[0]


def draw_doc_start(key, part):
    return document_plan(key)[1]


def draw_block_mask(key, part):
    return document_plan(key)[2]


def block_levels(rng, dims, shards, least, largest):
    level, own = 1.0, jax.random.fold_in(rng, 6)
    for dim, parts in shards:
        draws = jnp.exp(jax.random.uniform(jax.random.fold_in(own, dim), (parts,), jnp.float32, least / len(shards), largest / len(shards)))
        level = level * jnp.repeat(draws, dims[dim] // parts).reshape([-1 if axis == dim else 1 for axis in range(len(dims))])
    return level


def bell_draw(rng, dims, width, most, pieces=(), kind=jnp.bfloat16):
    array = jax.random.normal(rng, dims, jnp.float32) * width
    if len(pieces) > 0:
        array = block_levels(rng, dims, pieces, -0.22, 0.18) * array
    return jnp.clip(array, min=-most, max=most).astype(kind)


def setup_inputs(seed: int = 0) -> dict:
    arg_keys = jax.random.split(jax.random.key(seed), 9)
    return {
        "hidden": bell_draw(arg_keys[0], (MICRO, TOKENS, WIDTH), 1.0, 6.0, ((1, 64),)),
        "gain": jnp.clip(1.0 + 0.18 * jax.random.normal(arg_keys[1], (SECTIONS, WIDTH), jnp.float32), 0.1, 1.9),
        "keys": bell_draw(arg_keys[2], (SECTIONS, MICRO, TOKENS, KV_WIDTH), 1.0, 4.0, ((0, 4), (2, 64))),
        "values": bell_draw(arg_keys[3], (SECTIONS, MICRO, TOKENS, KV_WIDTH), 1.0, 6.0, ((0, 4), (2, 64))),
        "cotangent": bell_draw(arg_keys[4], (MICRO, DOCS, WIDTH), (MAXDOC // 4), 384.0, (), jnp.float32),
        "lengths": draw_lengths(jax.random.fold_in(arg_keys[8], 71), 0),
        "doc_start": draw_doc_start(jax.random.fold_in(arg_keys[8], 71), 0),
        "block_mask": draw_block_mask(jax.random.fold_in(arg_keys[8], 71), 0),
    }


NORM_EPS = 1e-05

def norm_rows(stream):
    values_f = stream.astype(jnp.float32)
    inv_rms = lax.rsqrt(lax.optimization_barrier(jnp.mean(values_f * values_f, axis=-1)) + NORM_EPS)
    return (values_f * inv_rms[:, None], inv_rms)

def scores_of(queries, key_rows, score_scale):
    return jnp.einsum('ikgd,jkd->kgij', queries.astype(jnp.float32), key_rows.astype(jnp.float32)) * score_scale

def reference(hidden, gain, keys, values, cotangent, lengths, doc_start, block_mask):
    group_share = HEADS // KV_HEADS
    score_scale = HEAD_DIM ** (-0.5)
    span_rows = SPAN * TOK_DEV
    wide_rows = span_rows + TOK_DEV
    stream_out = []
    keys_out = []
    values_out = []
    gain_out = [jnp.zeros((WIDTH,), jnp.float32) for segment in range(SECTIONS)]
    per_segment_stream = [[] for segment in range(SECTIONS)]
    per_segment_keys = [[] for segment in range(SECTIONS)]
    per_segment_values = [[] for segment in range(SECTIONS)]
    for microbatch_index in range(MICRO):
        starts_all = doc_start[microbatch_index]
        starts_pad = jnp.concatenate([-jnp.ones((span_rows,), jnp.int32), starts_all.astype(jnp.int32)])
        block_rows = block_mask[microbatch_index]

        def allowed_of(block):
            query_pos = block * TOK_DEV + jnp.arange(TOK_DEV, dtype=jnp.int32)
            key_pos = block * TOK_DEV - span_rows + jnp.arange(wide_rows, dtype=jnp.int32)
            block_of_keys = block - SPAN + jnp.arange(wide_rows, dtype=jnp.int32) // TOK_DEV
            active_flag = (block_of_keys >= 0) & (block_rows[block, jnp.maximum(block_of_keys, 0)] == 1)
            query_docs = lax.dynamic_slice_in_dim(starts_all, block * TOK_DEV, TOK_DEV)
            key_docs = lax.dynamic_slice_in_dim(starts_pad, block * TOK_DEV, wide_rows)
            return (query_docs[:, None] == key_docs[None, :]) & (query_pos[:, None] >= key_pos[None, :]) & active_flag[None, :]
        streams = [hidden[microbatch_index]]
        saved = []
        for segment in range(SECTIONS):
            stream_in = streams[-1]
            normed, inv_rms = norm_rows(stream_in)
            queries = (normed * gain[segment]).astype(jnp.bfloat16).reshape(TOKENS, KV_HEADS, group_share, HEAD_DIM)
            key_pad = jnp.concatenate([jnp.zeros((span_rows, KV_WIDTH), keys.dtype), keys[segment, microbatch_index]]).reshape(-1, KV_HEADS, HEAD_DIM)
            value_pad = jnp.concatenate([jnp.zeros((span_rows, KV_WIDTH), values.dtype), values[segment, microbatch_index]]).reshape(-1, KV_HEADS, HEAD_DIM)

            def forward_block(block, queries=queries, key_pad=key_pad, value_pad=value_pad):
                block_of_queries = lax.dynamic_slice_in_dim(queries, block * TOK_DEV, TOK_DEV)
                key_wide = lax.dynamic_slice_in_dim(key_pad, block * TOK_DEV, wide_rows)
                value_wide = lax.dynamic_slice_in_dim(value_pad, block * TOK_DEV, wide_rows)
                allowed = allowed_of(block)
                scores = scores_of(block_of_queries, key_wide, score_scale)
                exp_total = lax.optimization_barrier(jnp.sum(jnp.where(allowed, jnp.exp(scores), 0.0), axis=-1))
                log_total = jnp.log(exp_total)
                weights = jnp.where(allowed, jnp.exp(scores - log_total[..., None]), 0.0).astype(jnp.bfloat16)
                attended = jnp.einsum('kgij,jkd->ikgd', weights.astype(jnp.float32), value_wide.astype(jnp.float32))
                return (attended.astype(jnp.bfloat16), log_total)
            attended, log_total = lax.map(forward_block, jnp.arange(BLOCKS, dtype=jnp.int32))
            attended = attended.reshape(TOKENS, WIDTH)
            streams.append((stream_in.astype(jnp.float32) + attended.astype(jnp.float32)).astype(jnp.bfloat16))
            saved.append((queries, key_pad, value_pad, attended, log_total, normed, inv_rms))
        doc_lengths = lengths[microbatch_index]
        doc_ends = jnp.cumsum(doc_lengths)
        positions = jnp.arange(TOKENS, dtype=jnp.int32)
        doc_owner = lax.optimization_barrier(jnp.sum((positions[:, None] >= doc_ends[None, :]).astype(jnp.int32), axis=1))
        out_grad = (cotangent[microbatch_index][doc_owner] / doc_lengths[doc_owner].astype(jnp.float32)[:, None]).astype(jnp.bfloat16)
        for segment in reversed(range(SECTIONS)):
            queries, key_pad, value_pad, attended, log_total, normed, inv_rms = saved[segment]
            grad_four = out_grad.reshape(TOKENS, KV_HEADS, group_share, HEAD_DIM)
            attended_four = attended.reshape(TOKENS, KV_HEADS, group_share, HEAD_DIM)
            out_dot = jnp.transpose(lax.optimization_barrier(jnp.sum(grad_four.astype(jnp.float32) * attended_four.astype(jnp.float32), axis=-1)), (1, 2, 0))

            def backward_block(carried, block, queries=queries, key_pad=key_pad, value_pad=value_pad, grad_four=grad_four, out_dot=out_dot, log_total=log_total):
                key_pad_grad, value_pad_grad = carried
                block_of_queries = lax.dynamic_slice_in_dim(queries, block * TOK_DEV, TOK_DEV)
                grad_block = lax.dynamic_slice_in_dim(grad_four, block * TOK_DEV, TOK_DEV)
                key_wide = lax.dynamic_slice_in_dim(key_pad, block * TOK_DEV, wide_rows)
                value_wide = lax.dynamic_slice_in_dim(value_pad, block * TOK_DEV, wide_rows)
                dot_block = lax.dynamic_slice_in_dim(out_dot, block * TOK_DEV, TOK_DEV, axis=2)
                allowed = allowed_of(block)
                scores = scores_of(block_of_queries, key_wide, score_scale)
                probability = jnp.where(allowed, jnp.exp(scores - log_total[block][..., None]), 0.0)
                weights = probability.astype(jnp.bfloat16)
                prob_grad = jnp.einsum('ikgd,jkd->kgij', grad_block.astype(jnp.float32), value_wide.astype(jnp.float32))
                score_grad = (probability * (prob_grad - dot_block[..., None]) * score_scale).astype(jnp.bfloat16)
                query_grad = jnp.einsum('kgij,jkd->ikgd', score_grad.astype(jnp.float32), key_wide.astype(jnp.float32))
                key_grad = jnp.einsum('kgij,ikgd->jkd', score_grad.astype(jnp.float32), block_of_queries.astype(jnp.float32))
                value_grad = jnp.einsum('kgij,ikgd->jkd', weights.astype(jnp.float32), grad_block.astype(jnp.float32))
                old_keys = lax.dynamic_slice_in_dim(key_pad_grad, block * TOK_DEV, wide_rows)
                old_values = lax.dynamic_slice_in_dim(value_pad_grad, block * TOK_DEV, wide_rows)
                key_pad_grad = lax.dynamic_update_slice_in_dim(key_pad_grad, old_keys + key_grad, block * TOK_DEV, 0)
                value_pad_grad = lax.dynamic_update_slice_in_dim(value_pad_grad, old_values + value_grad, block * TOK_DEV, 0)
                return ((key_pad_grad, value_pad_grad), query_grad)
            initial = (jnp.zeros((TOKENS + span_rows, KV_HEADS, HEAD_DIM), jnp.float32), jnp.zeros((TOKENS + span_rows, KV_HEADS, HEAD_DIM), jnp.float32))
            (key_pad_grad, value_pad_grad), query_grad = lax.scan(backward_block, initial, jnp.arange(BLOCKS, dtype=jnp.int32))
            query_grad = query_grad.reshape(TOKENS, WIDTH)
            gain_out[segment] = gain_out[segment] + lax.optimization_barrier(jnp.sum(query_grad * normed, axis=0))
            normed_grad = query_grad * gain[segment]
            norm_grad = inv_rms[:, None] * (normed_grad - normed * lax.optimization_barrier(jnp.mean(normed_grad * normed, axis=-1, keepdims=True)))
            out_grad = (out_grad.astype(jnp.float32) + norm_grad).astype(jnp.bfloat16)
            per_segment_stream[segment].append(out_grad)
            per_segment_keys[segment].append(key_pad_grad[span_rows:].reshape(TOKENS, KV_WIDTH).astype(jnp.bfloat16))
            per_segment_values[segment].append(value_pad_grad[span_rows:].reshape(TOKENS, KV_WIDTH).astype(jnp.bfloat16))
    for segment in range(SECTIONS):
        stream_out.append(jnp.stack(per_segment_stream[segment]))
        keys_out.append(jnp.stack(per_segment_keys[segment]))
        values_out.append(jnp.stack(per_segment_values[segment]))
    return (jnp.stack(stream_out), jnp.stack(keys_out), jnp.stack(values_out), jnp.stack(gain_out))
```

```python
import jax
import jax.numpy as jnp
from jax import lax
from jax.sharding import PartitionSpec as P

HEAD_DIM = 128
SPAN = 2


NORM_EPS = 1e-05


def shifted(x, axis, by):
    size = lax.axis_size(axis)
    pairs = [(i, i + by) for i in range(size) if 0 <= i + by < size]
    return lax.ppermute(x, axis, pairs)


def butterfly_sum(x, axis):
    size = lax.axis_size(axis)
    if size & (size - 1):
        return lax.psum(x, axis)
    step = 1
    while step < size:
        pairs = [(i, i ^ step) for i in range(size)]
        x = x + lax.ppermute(x, axis, pairs)
        step *= 2
    return x


def norm_rows(stream):
    values_f = stream.astype(jnp.float32)
    inv_rms = lax.rsqrt(jnp.mean(values_f * values_f, axis=-1) + NORM_EPS)
    return (values_f * inv_rms[:, None], inv_rms)


def per_device(hidden, gain, keys, values, cotangent, lengths, doc_start, block_mask):
    section = lax.axis_index("pipe")
    segment_count = lax.axis_size("pipe")
    index_of_block = lax.axis_index("ctx")
    micro_count, tok_rows, feat_width = hidden.shape
    kv_width = keys.shape[3]
    groups = kv_width // HEAD_DIM
    group_share = feat_width // HEAD_DIM // groups
    score_scale = HEAD_DIM ** (-0.5)
    gain_row = gain[0]
    last_segment = segment_count - 1
    offsets = jnp.arange(tok_rows, dtype=jnp.int32)
    own_pos = index_of_block * tok_rows + offsets
    wide_rows = (SPAN + 1) * tok_rows
    key_pos = (index_of_block - SPAN) * tok_rows + jnp.arange(wide_rows, dtype=jnp.int32)
    time_steps = micro_count + segment_count - 1
    four_shape = (tok_rows, groups, group_share, HEAD_DIM)

    kv_own = jnp.concatenate([keys[0], values[0]], axis=-1)
    kv_parts = [shifted(kv_own, "ctx", distance) for distance in range(SPAN, 0, -1)] + [kv_own]
    kv_wide = jnp.concatenate(kv_parts, axis=1)
    key_wide = [
        kv_wide[m, :, :kv_width].reshape(wide_rows, groups, HEAD_DIM) for m in range(micro_count)
    ]
    value_wide = [
        kv_wide[m, :, kv_width:].reshape(wide_rows, groups, HEAD_DIM) for m in range(micro_count)
    ]
    allowed_all = [
        (key_pos[None, :] >= doc_start[m][:, None]) & (key_pos[None, :] <= own_pos[:, None])
        for m in range(micro_count)
    ]

    def pick(items, index):
        out = items[0]
        for m in range(1, len(items)):
            out = jnp.where(index == m, items[m], out)
        return out

    received = jnp.zeros((tok_rows, feat_width), jnp.bfloat16)
    stream_store = [jnp.zeros((tok_rows, feat_width), jnp.bfloat16) for _ in range(micro_count)]
    attended_store = [jnp.zeros((tok_rows, feat_width), jnp.bfloat16) for _ in range(micro_count)]
    log_store = [
        jnp.zeros((groups, group_share, tok_rows), jnp.float32) for _ in range(micro_count)
    ]
    for time_step in range(time_steps):
        raw_index = time_step - section
        working_buffer = (raw_index >= 0) & (raw_index < micro_count)
        microbatch_index = jnp.clip(raw_index, 0, micro_count - 1)
        stream_in = jnp.where(section == 0, hidden[microbatch_index], received)
        key_rows = pick(key_wide, microbatch_index)
        value_rows = pick(value_wide, microbatch_index)
        allowed = pick(allowed_all, microbatch_index)
        normed, inv_rms = norm_rows(stream_in)
        queries = (normed * gain_row).astype(jnp.bfloat16).reshape(four_shape)
        scores = (
            jnp.einsum("ikgd,jkd->kgij", queries, key_rows, preferred_element_type=jnp.float32)
            * score_scale
        )
        total_sum = jnp.sum(jnp.where(allowed, jnp.exp(scores), 0.0), axis=-1)
        log_total = jnp.log(total_sum)
        weights = jnp.where(allowed, jnp.exp(scores - log_total[..., None]), 0.0).astype(
            jnp.bfloat16
        )
        out_sum = jnp.einsum(
            "kgij,jkd->ikgd", weights, value_rows, preferred_element_type=jnp.float32
        )
        attended = out_sum.reshape(tok_rows, feat_width).astype(jnp.bfloat16)
        stream_out = (stream_in.astype(jnp.float32) + attended.astype(jnp.float32)).astype(
            jnp.bfloat16
        )
        for m in range(micro_count):
            hit = working_buffer & (microbatch_index == m)
            stream_store[m] = jnp.where(hit, stream_in, stream_store[m])
            attended_store[m] = jnp.where(hit, attended, attended_store[m])
            log_store[m] = jnp.where(hit, log_total, log_store[m])
        if time_step < time_steps - 1:
            received = shifted(stream_out, "pipe", 1)

    doc_ends = jnp.cumsum(lengths, axis=1)
    doc_starts = doc_ends - lengths
    seeds = []
    for m in range(micro_count):
        onehot = (
            (own_pos[:, None] >= doc_starts[m][None, :]) & (own_pos[:, None] < doc_ends[m][None, :])
        ).astype(jnp.float32)
        picked = jnp.dot(onehot, cotangent[m], precision=lax.Precision.HIGHEST)
        doc_length = jnp.dot(
            onehot, lengths[m].astype(jnp.float32), precision=lax.Precision.HIGHEST
        )
        seeds.append((picked / doc_length[:, None]).astype(jnp.bfloat16))

    received = jnp.zeros((tok_rows, feat_width), jnp.bfloat16)
    grad_stream = [jnp.zeros((tok_rows, feat_width), jnp.bfloat16) for _ in range(micro_count)]
    kv_total = [jnp.zeros((tok_rows, 2 * kv_width), jnp.float32) for _ in range(micro_count)]
    kv_sent = [
        [jnp.zeros((tok_rows, 2 * kv_width), jnp.bfloat16) for _ in range(micro_count)]
        for _ in range(SPAN)
    ]
    gain_total = jnp.zeros((feat_width,), jnp.float32)
    for time_step in range(time_steps):
        raw_index = time_step - (last_segment - section)
        working_buffer = (raw_index >= 0) & (raw_index < micro_count)
        microbatch_index = jnp.clip(raw_index, 0, micro_count - 1)
        out_grad = jnp.where(section == last_segment, pick(seeds, microbatch_index), received)
        key_rows = pick(key_wide, microbatch_index)
        value_rows = pick(value_wide, microbatch_index)
        allowed = pick(allowed_all, microbatch_index)
        stream_in = pick(stream_store, microbatch_index)
        normed, inv_rms = norm_rows(stream_in)
        queries = (normed * gain_row).astype(jnp.bfloat16).reshape(four_shape)
        grad_four = out_grad.reshape(four_shape)
        attended_four = pick(attended_store, microbatch_index).reshape(four_shape)
        out_dot = jnp.transpose(
            jnp.sum(grad_four.astype(jnp.float32) * attended_four.astype(jnp.float32), axis=-1),
            (1, 2, 0),
        )
        log_total = pick(log_store, microbatch_index)
        scores = (
            jnp.einsum("ikgd,jkd->kgij", queries, key_rows, preferred_element_type=jnp.float32)
            * score_scale
        )
        probability = jnp.where(allowed, jnp.exp(scores - log_total[..., None]), 0.0)
        prob_grad = jnp.einsum(
            "ikgd,jkd->kgij", grad_four, value_rows, preferred_element_type=jnp.float32
        )
        score_grad = (probability * (prob_grad - out_dot[..., None]) * score_scale).astype(
            jnp.bfloat16
        )
        weights = probability.astype(jnp.bfloat16)
        query_grad = jnp.einsum(
            "kgij,jkd->ikgd", score_grad, key_rows, preferred_element_type=jnp.float32
        )
        key_grad = jnp.einsum(
            "kgij,ikgd->jkd", score_grad, queries, preferred_element_type=jnp.float32
        ).reshape(wide_rows, kv_width)
        value_grad = jnp.einsum(
            "kgij,ikgd->jkd", weights, grad_four, preferred_element_type=jnp.float32
        ).reshape(wide_rows, kv_width)
        kv_grad = jnp.concatenate([key_grad, value_grad], axis=-1)
        for m in range(micro_count):
            hit = working_buffer & (microbatch_index == m)
            kv_total[m] = jnp.where(hit, kv_grad[SPAN * tok_rows :], kv_total[m])
            for distance in range(1, SPAN + 1):
                lo = (SPAN - distance) * tok_rows
                kv_sent[distance - 1][m] = jnp.where(
                    hit,
                    kv_grad[lo : lo + tok_rows].astype(jnp.bfloat16),
                    kv_sent[distance - 1][m],
                )
        grad_flat = query_grad.reshape(tok_rows, feat_width)
        gain_total = gain_total + jnp.where(
            working_buffer, jnp.sum(grad_flat * normed, axis=0), 0.0
        )
        normed_grad = grad_flat * gain_row
        norm_grad = inv_rms[:, None] * (
            normed_grad - normed * jnp.mean(normed_grad * normed, axis=-1, keepdims=True)
        )
        stream_grad = (out_grad.astype(jnp.float32) + norm_grad).astype(jnp.bfloat16)
        for m in range(micro_count):
            hit = working_buffer & (microbatch_index == m)
            grad_stream[m] = jnp.where(hit, stream_grad, grad_stream[m])
        if time_step < time_steps - 1:
            received = shifted(stream_grad, "pipe", -1)

    kv_out = jnp.stack(kv_total)
    for distance in range(1, SPAN + 1):
        returned = shifted(jnp.stack(kv_sent[distance - 1]), "ctx", -distance)
        kv_out = kv_out + returned.astype(jnp.float32)
    kv_out = kv_out.astype(jnp.bfloat16)
    gain_sum = butterfly_sum(gain_total, "ctx")
    return (
        jnp.stack(grad_stream)[None],
        kv_out[:, :, :kv_width][None],
        kv_out[:, :, kv_width:][None],
        gain_sum.reshape(1, feat_width),
    )


def solution(mesh):
    placed = (
        P(None, "ctx", None),
        P("pipe", None),
        P("pipe", None, "ctx", None),
        P("pipe", None, "ctx", None),
        P(),
        P(),
        P(None, "ctx"),
        P(),
    )
    return jax.shard_map(
        per_device,
        mesh=mesh,
        in_specs=placed,
        out_specs=(
            P("pipe", None, "ctx", None),
            P("pipe", None, "ctx", None),
            P("pipe", None, "ctx", None),
            P("pipe", None),
        ),
        check_vma=False,
    )
```

```python
import functools

import jax
import jax.numpy as jnp
from jax import lax
from jax.experimental import pallas as pl
from jax.sharding import PartitionSpec as P

HEAD_DIM = 128
SPAN = 2


NORM_EPS = 1e-05


def shifted(x, axis, by):
    size = lax.axis_size(axis)
    pairs = [(i, i + by) for i in range(size) if 0 <= i + by < size]
    return lax.ppermute(x, axis, pairs)


def butterfly_sum(x, axis):
    size = lax.axis_size(axis)
    if size & (size - 1):
        return lax.psum(x, axis)
    step = 1
    while step < size:
        pairs = [(i, i ^ step) for i in range(size)]
        x = x + lax.ppermute(x, axis, pairs)
        step *= 2
    return x

NT = (((1,), (1,)), ((), ()))
TN = (((0,), (0,)), ((), ()))

def fwd_kernel(q_ref, k_ref, v_ref, lo_ref, hi_ref, kp_ref, o_ref, lt_ref, *, heads, share, scale):
    kpos = kp_ref[...]
    allowed = (kpos >= lo_ref[...]) & (kpos <= hi_ref[...])
    for h in range(heads):
        g = h // share
        hs = slice(h * HEAD_DIM, (h + 1) * HEAD_DIM)
        gs = slice(g * HEAD_DIM, (g + 1) * HEAD_DIM)
        s = lax.dot_general(q_ref[:, hs], k_ref[:, gs], NT, preferred_element_type=jnp.float32) * scale
        tot = jnp.sum(jnp.where(allowed, jnp.exp(s), 0.0), axis=1, keepdims=True)
        lt = jnp.log(tot)
        w = jnp.where(allowed, jnp.exp(s - lt), 0.0).astype(jnp.bfloat16)
        o = jnp.dot(w, v_ref[:, gs], preferred_element_type=jnp.float32)
        o_ref[:, hs] = o.astype(o_ref.dtype)
        lt_ref[:, h:h + 1] = lt

def bwd_kernel(q_ref, do_ref, att_ref, k_ref, v_ref, lt_ref, lo_ref, hi_ref, kp_ref, dq_ref, dk_ref, dv_ref, *, heads, share, scale):
    kpos = kp_ref[...]
    allowed = (kpos >= lo_ref[...]) & (kpos <= hi_ref[...])
    for g in range(heads // share):
        gs = slice(g * HEAD_DIM, (g + 1) * HEAD_DIM)
        k = k_ref[:, gs]
        v = v_ref[:, gs]
        dk = None
        dv = None
        for h in range(g * share, (g + 1) * share):
            hs = slice(h * HEAD_DIM, (h + 1) * HEAD_DIM)
            q = q_ref[:, hs]
            do = do_ref[:, hs]
            od = jnp.sum(do.astype(jnp.float32) * att_ref[:, hs].astype(jnp.float32), axis=1, keepdims=True)
            s = lax.dot_general(q, k, NT, preferred_element_type=jnp.float32) * scale
            p = jnp.where(allowed, jnp.exp(s - lt_ref[:, h:h + 1]), 0.0)
            dp = lax.dot_general(do, v, NT, preferred_element_type=jnp.float32)
            ds = (p * (dp - od) * scale).astype(jnp.bfloat16)
            w = p.astype(jnp.bfloat16)
            dq_ref[:, hs] = jnp.dot(ds, k, preferred_element_type=jnp.float32)
            dkh = lax.dot_general(ds, q, TN, preferred_element_type=jnp.float32)
            dvh = lax.dot_general(w, do, TN, preferred_element_type=jnp.float32)
            dk = dkh if dk is None else dk + dkh
            dv = dvh if dv is None else dv + dvh
        dk_ref[:, gs] = dk
        dv_ref[:, gs] = dv

def attn_fwd(q, k, v, lo, hi, kp):
    rows, width = q.shape
    heads = width // HEAD_DIM
    share = heads // (k.shape[1] // HEAD_DIM)
    kern = functools.partial(fwd_kernel, heads=heads, share=share, scale=HEAD_DIM ** -0.5)
    return pl.pallas_call(kern, out_shape=(jax.ShapeDtypeStruct((rows, width), jnp.bfloat16), jax.ShapeDtypeStruct((rows, heads), jnp.float32)))(q, k, v, lo, hi, kp)

def attn_bwd(q, do, att, k, v, lt, lo, hi, kp):
    rows, width = q.shape
    heads = width // HEAD_DIM
    share = heads // (k.shape[1] // HEAD_DIM)
    kern = functools.partial(bwd_kernel, heads=heads, share=share, scale=HEAD_DIM ** -0.5)
    return pl.pallas_call(kern, out_shape=(jax.ShapeDtypeStruct((rows, width), jnp.float32), jax.ShapeDtypeStruct(k.shape, jnp.float32), jax.ShapeDtypeStruct(v.shape, jnp.float32)))(q, do, att, k, v, lt, lo, hi, kp)


def norm_rows(stream):
    values_f = stream.astype(jnp.float32)
    inv_rms = lax.rsqrt(jnp.mean(values_f * values_f, axis=-1) + NORM_EPS)
    return (values_f * inv_rms[:, None], inv_rms)


def per_device(hidden, gain, keys, values, cotangent, lengths, doc_start, block_mask):
    section = lax.axis_index("pipe")
    segment_count = lax.axis_size("pipe")
    index_of_block = lax.axis_index("ctx")
    micro_count, tok_rows, feat_width = hidden.shape
    kv_width = keys.shape[3]
    groups = kv_width // HEAD_DIM
    group_share = feat_width // HEAD_DIM // groups
    score_scale = HEAD_DIM ** (-0.5)
    gain_row = gain[0]
    last_segment = segment_count - 1
    offsets = jnp.arange(tok_rows, dtype=jnp.int32)
    own_pos = index_of_block * tok_rows + offsets
    wide_rows = (SPAN + 1) * tok_rows
    key_pos = (index_of_block - SPAN) * tok_rows + jnp.arange(wide_rows, dtype=jnp.int32)
    time_steps = micro_count + segment_count - 1
    four_shape = (tok_rows, groups, group_share, HEAD_DIM)

    kv_own = jnp.concatenate([keys[0], values[0]], axis=-1)
    kv_parts = [shifted(kv_own, "ctx", distance) for distance in range(SPAN, 0, -1)] + [kv_own]
    kv_wide = jnp.concatenate(kv_parts, axis=1)
    key_wide = [kv_wide[m, :, :kv_width] for m in range(micro_count)]
    value_wide = [kv_wide[m, :, kv_width:] for m in range(micro_count)]
    lower_all = [doc_start[m][:, None] for m in range(micro_count)]
    upper = own_pos[:, None]
    key_row = key_pos[None, :]

    def pick(items, index):
        out = items[0]
        for m in range(1, len(items)):
            out = jnp.where(index == m, items[m], out)
        return out

    received = jnp.zeros((tok_rows, feat_width), jnp.bfloat16)
    stream_store = [jnp.zeros((tok_rows, feat_width), jnp.bfloat16) for _ in range(micro_count)]
    attended_store = [jnp.zeros((tok_rows, feat_width), jnp.bfloat16) for _ in range(micro_count)]
    log_store = [
        jnp.zeros((tok_rows, groups * group_share), jnp.float32) for _ in range(micro_count)
    ]
    for time_step in range(time_steps):
        raw_index = time_step - section
        working_buffer = (raw_index >= 0) & (raw_index < micro_count)
        microbatch_index = jnp.clip(raw_index, 0, micro_count - 1)
        stream_in = jnp.where(section == 0, hidden[microbatch_index], received)
        key_rows = pick(key_wide, microbatch_index)
        value_rows = pick(value_wide, microbatch_index)
        lower = pick(lower_all, microbatch_index)
        normed, inv_rms = norm_rows(stream_in)
        queries = (normed * gain_row).astype(jnp.bfloat16)
        attended, log_total = attn_fwd(queries, key_rows, value_rows, lower, upper, key_row)
        stream_out = (stream_in.astype(jnp.float32) + attended.astype(jnp.float32)).astype(
            jnp.bfloat16
        )
        for m in range(micro_count):
            hit = working_buffer & (microbatch_index == m)
            stream_store[m] = jnp.where(hit, stream_in, stream_store[m])
            attended_store[m] = jnp.where(hit, attended, attended_store[m])
            log_store[m] = jnp.where(hit, log_total, log_store[m])
        if time_step < time_steps - 1:
            received = shifted(stream_out, "pipe", 1)

    doc_ends = jnp.cumsum(lengths, axis=1)
    doc_starts = doc_ends - lengths
    seeds = []
    for m in range(micro_count):
        onehot = (
            (own_pos[:, None] >= doc_starts[m][None, :]) & (own_pos[:, None] < doc_ends[m][None, :])
        ).astype(jnp.float32)
        picked = jnp.dot(onehot, cotangent[m], precision=lax.Precision.HIGHEST)
        doc_length = jnp.dot(
            onehot, lengths[m].astype(jnp.float32), precision=lax.Precision.HIGHEST
        )
        seeds.append((picked / doc_length[:, None]).astype(jnp.bfloat16))

    received = jnp.zeros((tok_rows, feat_width), jnp.bfloat16)
    grad_stream = [jnp.zeros((tok_rows, feat_width), jnp.bfloat16) for _ in range(micro_count)]
    kv_total = [jnp.zeros((tok_rows, 2 * kv_width), jnp.float32) for _ in range(micro_count)]
    kv_sent = [
        [jnp.zeros((tok_rows, 2 * kv_width), jnp.bfloat16) for _ in range(micro_count)]
        for _ in range(SPAN)
    ]
    gain_total = jnp.zeros((feat_width,), jnp.float32)
    for time_step in range(time_steps):
        raw_index = time_step - (last_segment - section)
        working_buffer = (raw_index >= 0) & (raw_index < micro_count)
        microbatch_index = jnp.clip(raw_index, 0, micro_count - 1)
        out_grad = jnp.where(section == last_segment, pick(seeds, microbatch_index), received)
        key_rows = pick(key_wide, microbatch_index)
        value_rows = pick(value_wide, microbatch_index)
        lower = pick(lower_all, microbatch_index)
        stream_in = pick(stream_store, microbatch_index)
        normed, inv_rms = norm_rows(stream_in)
        queries = (normed * gain_row).astype(jnp.bfloat16)
        log_total = pick(log_store, microbatch_index)
        query_grad, key_grad, value_grad = attn_bwd(
            queries,
            out_grad,
            pick(attended_store, microbatch_index),
            key_rows,
            value_rows,
            log_total,
            lower,
            upper,
            key_row,
        )
        kv_grad = jnp.concatenate([key_grad, value_grad], axis=-1)
        for m in range(micro_count):
            hit = working_buffer & (microbatch_index == m)
            kv_total[m] = jnp.where(hit, kv_grad[SPAN * tok_rows :], kv_total[m])
            for distance in range(1, SPAN + 1):
                lo = (SPAN - distance) * tok_rows
                kv_sent[distance - 1][m] = jnp.where(
                    hit,
                    kv_grad[lo : lo + tok_rows].astype(jnp.bfloat16),
                    kv_sent[distance - 1][m],
                )
        grad_flat = query_grad.reshape(tok_rows, feat_width)
        gain_total = gain_total + jnp.where(
            working_buffer, jnp.sum(grad_flat * normed, axis=0), 0.0
        )
        normed_grad = grad_flat * gain_row
        norm_grad = inv_rms[:, None] * (
            normed_grad - normed * jnp.mean(normed_grad * normed, axis=-1, keepdims=True)
        )
        stream_grad = (out_grad.astype(jnp.float32) + norm_grad).astype(jnp.bfloat16)
        for m in range(micro_count):
            hit = working_buffer & (microbatch_index == m)
            grad_stream[m] = jnp.where(hit, stream_grad, grad_stream[m])
        if time_step < time_steps - 1:
            received = shifted(stream_grad, "pipe", -1)

    kv_out = jnp.stack(kv_total)
    for distance in range(1, SPAN + 1):
        returned = shifted(jnp.stack(kv_sent[distance - 1]), "ctx", -distance)
        kv_out = kv_out + returned.astype(jnp.float32)
    kv_out = kv_out.astype(jnp.bfloat16)
    gain_sum = butterfly_sum(gain_total, "ctx")
    return (
        jnp.stack(grad_stream)[None],
        kv_out[:, :, :kv_width][None],
        kv_out[:, :, kv_width:][None],
        gain_sum.reshape(1, feat_width),
    )


def solution(mesh):
    placed = (
        P(None, "ctx", None),
        P("pipe", None),
        P("pipe", None, "ctx", None),
        P("pipe", None, "ctx", None),
        P(),
        P(),
        P(None, "ctx"),
        P(),
    )
    return jax.shard_map(
        per_device,
        mesh=mesh,
        in_specs=placed,
        out_specs=(
            P("pipe", None, "ctx", None),
            P("pipe", None, "ctx", None),
            P("pipe", None, "ctx", None),
            P("pipe", None),
        ),
        check_vma=False,
    )
```

```python
import functools

import jax
import jax.numpy as jnp
from jax import lax
from jax.experimental import pallas as pl
from jax.sharding import PartitionSpec as P

HEAD_DIM = 128
SPAN = 2
CHUNKS = 2


NORM_EPS = 1e-05


def shifted(x, axis, by):
    size = lax.axis_size(axis)
    pairs = [(i, i + by) for i in range(size) if 0 <= i + by < size]
    return lax.ppermute(x, axis, pairs)


def butterfly_sum(x, axis):
    size = lax.axis_size(axis)
    if size & (size - 1):
        return lax.psum(x, axis)
    step = 1
    while step < size:
        pairs = [(i, i ^ step) for i in range(size)]
        x = x + lax.ppermute(x, axis, pairs)
        step *= 2
    return x

NT = (((1,), (1,)), ((), ()))
TN = (((0,), (0,)), ((), ()))

def fwd_kernel(q_ref, k_ref, v_ref, lo_ref, hi_ref, kp_ref, o_ref, lt_ref, *, heads, share, scale):
    kpos = kp_ref[...]
    allowed = (kpos >= lo_ref[...]) & (kpos <= hi_ref[...])
    for h in range(heads):
        g = h // share
        hs = slice(h * HEAD_DIM, (h + 1) * HEAD_DIM)
        gs = slice(g * HEAD_DIM, (g + 1) * HEAD_DIM)
        s = lax.dot_general(q_ref[:, hs], k_ref[:, gs], NT, preferred_element_type=jnp.float32) * scale
        tot = jnp.sum(jnp.where(allowed, jnp.exp(s), 0.0), axis=1, keepdims=True)
        lt = jnp.log(tot)
        w = jnp.where(allowed, jnp.exp(s - lt), 0.0).astype(jnp.bfloat16)
        o = jnp.dot(w, v_ref[:, gs], preferred_element_type=jnp.float32)
        o_ref[:, hs] = o.astype(o_ref.dtype)
        lt_ref[:, h:h + 1] = lt

def bwd_kernel(q_ref, do_ref, att_ref, k_ref, v_ref, lt_ref, lo_ref, hi_ref, kp_ref, dq_ref, dk_ref, dv_ref, *, heads, share, scale):
    kpos = kp_ref[...]
    allowed = (kpos >= lo_ref[...]) & (kpos <= hi_ref[...])
    for g in range(heads // share):
        gs = slice(g * HEAD_DIM, (g + 1) * HEAD_DIM)
        k = k_ref[:, gs]
        v = v_ref[:, gs]
        dk = None
        dv = None
        for h in range(g * share, (g + 1) * share):
            hs = slice(h * HEAD_DIM, (h + 1) * HEAD_DIM)
            q = q_ref[:, hs]
            do = do_ref[:, hs]
            od = jnp.sum(do.astype(jnp.float32) * att_ref[:, hs].astype(jnp.float32), axis=1, keepdims=True)
            s = lax.dot_general(q, k, NT, preferred_element_type=jnp.float32) * scale
            p = jnp.where(allowed, jnp.exp(s - lt_ref[:, h:h + 1]), 0.0)
            dp = lax.dot_general(do, v, NT, preferred_element_type=jnp.float32)
            ds = (p * (dp - od) * scale).astype(jnp.bfloat16)
            w = p.astype(jnp.bfloat16)
            dq_ref[:, hs] = jnp.dot(ds, k, preferred_element_type=jnp.float32)
            dkh = lax.dot_general(ds, q, TN, preferred_element_type=jnp.float32)
            dvh = lax.dot_general(w, do, TN, preferred_element_type=jnp.float32)
            dk = dkh if dk is None else dk + dkh
            dv = dvh if dv is None else dv + dvh
        dk_ref[:, gs] = dk
        dv_ref[:, gs] = dv

def attn_fwd(q, k, v, lo, hi, kp):
    rows, width = q.shape
    heads = width // HEAD_DIM
    share = heads // (k.shape[1] // HEAD_DIM)
    kern = functools.partial(fwd_kernel, heads=heads, share=share, scale=HEAD_DIM ** -0.5)
    return pl.pallas_call(kern, out_shape=(jax.ShapeDtypeStruct((rows, width), jnp.bfloat16), jax.ShapeDtypeStruct((rows, heads), jnp.float32)))(q, k, v, lo, hi, kp)

def attn_bwd(q, do, att, k, v, lt, lo, hi, kp):
    rows, width = q.shape
    heads = width // HEAD_DIM
    share = heads // (k.shape[1] // HEAD_DIM)
    kern = functools.partial(bwd_kernel, heads=heads, share=share, scale=HEAD_DIM ** -0.5)
    return pl.pallas_call(kern, out_shape=(jax.ShapeDtypeStruct((rows, width), jnp.float32), jax.ShapeDtypeStruct(k.shape, jnp.float32), jax.ShapeDtypeStruct(v.shape, jnp.float32)))(q, do, att, k, v, lt, lo, hi, kp)


def norm_rows(stream):
    values_f = stream.astype(jnp.float32)
    inv_rms = lax.rsqrt(jnp.mean(values_f * values_f, axis=-1) + NORM_EPS)
    return (values_f * inv_rms[:, None], inv_rms)


def per_device(hidden, gain, keys, values, cotangent, lengths, doc_start, block_mask):
    section = lax.axis_index("pipe")
    segment_count = lax.axis_size("pipe")
    index_of_block = lax.axis_index("ctx")
    micro_count, tok_rows, feat_width = hidden.shape
    kv_width = keys.shape[3]
    groups = kv_width // HEAD_DIM
    group_share = feat_width // HEAD_DIM // groups
    gain_row = gain[0]
    last_segment = segment_count - 1
    offsets = jnp.arange(tok_rows, dtype=jnp.int32)
    own_pos = index_of_block * tok_rows + offsets
    wide_rows = (SPAN + 1) * tok_rows
    key_pos = (index_of_block - SPAN) * tok_rows + jnp.arange(wide_rows, dtype=jnp.int32)
    time_steps = micro_count + segment_count - 1

    kv_own = jnp.concatenate([keys[0], values[0]], axis=-1)
    kv_parts = [shifted(kv_own, "ctx", distance) for distance in range(SPAN, 0, -1)] + [kv_own]
    kv_wide = jnp.concatenate(kv_parts, axis=1)
    key_wide = [kv_wide[m, :, :kv_width] for m in range(micro_count)]
    value_wide = [kv_wide[m, :, kv_width:] for m in range(micro_count)]
    lower_all = [doc_start[m][:, None] for m in range(micro_count)]
    upper = own_pos[:, None]
    key_row = key_pos[None, :]

    def pick(items, index):
        out = items[0]
        for m in range(1, len(items)):
            out = jnp.where(index == m, items[m], out)
        return out

    chunk_rows = tok_rows // CHUNKS
    cuts = [slice(c * chunk_rows, (c + 1) * chunk_rows) for c in range(CHUNKS)]
    received = [jnp.zeros((chunk_rows, feat_width), jnp.bfloat16) for _ in range(CHUNKS)]
    blank = lambda shape, kind: [[jnp.zeros(shape, kind) for _ in range(CHUNKS)] for _ in range(micro_count)]
    stream_store = blank((chunk_rows, feat_width), jnp.bfloat16)
    attended_store = blank((chunk_rows, feat_width), jnp.bfloat16)
    log_store = blank((chunk_rows, groups * group_share), jnp.float32)
    for time_step in range(time_steps):
        raw_index = time_step - section
        working_buffer = (raw_index >= 0) & (raw_index < micro_count)
        microbatch_index = jnp.clip(raw_index, 0, micro_count - 1)
        key_rows = pick(key_wide, microbatch_index)
        value_rows = pick(value_wide, microbatch_index)
        lower = pick(lower_all, microbatch_index)
        hidden_in = hidden[microbatch_index]
        for c, cut in enumerate(cuts):
            stream_in = jnp.where(section == 0, hidden_in[cut], received[c])
            normed, inv_rms = norm_rows(stream_in)
            queries = (normed * gain_row).astype(jnp.bfloat16)
            attended, log_total = attn_fwd(
                queries, key_rows, value_rows, lower[cut], upper[cut], key_row
            )
            stream_out = (stream_in.astype(jnp.float32) + attended.astype(jnp.float32)).astype(
                jnp.bfloat16
            )
            for m in range(micro_count):
                hit = working_buffer & (microbatch_index == m)
                stream_store[m][c] = jnp.where(hit, stream_in, stream_store[m][c])
                attended_store[m][c] = jnp.where(hit, attended, attended_store[m][c])
                log_store[m][c] = jnp.where(hit, log_total, log_store[m][c])
            if time_step < time_steps - 1:
                received[c] = shifted(stream_out, "pipe", 1)

    doc_ends = jnp.cumsum(lengths, axis=1)
    doc_starts = doc_ends - lengths
    seeds = []
    for m in range(micro_count):
        onehot = (
            (own_pos[:, None] >= doc_starts[m][None, :]) & (own_pos[:, None] < doc_ends[m][None, :])
        ).astype(jnp.float32)
        picked = jnp.dot(onehot, cotangent[m], precision=lax.Precision.HIGHEST)
        doc_length = jnp.dot(
            onehot, lengths[m].astype(jnp.float32), precision=lax.Precision.HIGHEST
        )
        seeds.append((picked / doc_length[:, None]).astype(jnp.bfloat16))

    received = [jnp.zeros((chunk_rows, feat_width), jnp.bfloat16) for _ in range(CHUNKS)]
    grad_stream = blank((chunk_rows, feat_width), jnp.bfloat16)
    kv_total = [jnp.zeros((tok_rows, 2 * kv_width), jnp.float32) for _ in range(micro_count)]
    kv_sent = [
        [jnp.zeros((tok_rows, 2 * kv_width), jnp.bfloat16) for _ in range(micro_count)]
        for _ in range(SPAN)
    ]
    gain_total = jnp.zeros((feat_width,), jnp.float32)
    for time_step in range(time_steps):
        raw_index = time_step - (last_segment - section)
        working_buffer = (raw_index >= 0) & (raw_index < micro_count)
        microbatch_index = jnp.clip(raw_index, 0, micro_count - 1)
        key_rows = pick(key_wide, microbatch_index)
        value_rows = pick(value_wide, microbatch_index)
        lower = pick(lower_all, microbatch_index)
        seed = pick(seeds, microbatch_index)
        kv_grad = None
        for c, cut in enumerate(cuts):
            out_grad = jnp.where(section == last_segment, seed[cut], received[c])
            stream_in = pick([stream_store[m][c] for m in range(micro_count)], microbatch_index)
            normed, inv_rms = norm_rows(stream_in)
            queries = (normed * gain_row).astype(jnp.bfloat16)
            query_grad, key_grad, value_grad = attn_bwd(
                queries,
                out_grad,
                pick([attended_store[m][c] for m in range(micro_count)], microbatch_index),
                key_rows,
                value_rows,
                pick([log_store[m][c] for m in range(micro_count)], microbatch_index),
                lower[cut],
                upper[cut],
                key_row,
            )
            part = jnp.concatenate([key_grad, value_grad], axis=-1)
            kv_grad = part if kv_grad is None else kv_grad + part
            gain_total = gain_total + jnp.where(
                working_buffer, jnp.sum(query_grad * normed, axis=0), 0.0
            )
            normed_grad = query_grad * gain_row
            norm_grad = inv_rms[:, None] * (
                normed_grad - normed * jnp.mean(normed_grad * normed, axis=-1, keepdims=True)
            )
            stream_grad = (out_grad.astype(jnp.float32) + norm_grad).astype(jnp.bfloat16)
            for m in range(micro_count):
                hit = working_buffer & (microbatch_index == m)
                grad_stream[m][c] = jnp.where(hit, stream_grad, grad_stream[m][c])
            if time_step < time_steps - 1:
                received[c] = shifted(stream_grad, "pipe", -1)
        for m in range(micro_count):
            hit = working_buffer & (microbatch_index == m)
            kv_total[m] = jnp.where(hit, kv_grad[SPAN * tok_rows :], kv_total[m])
            for distance in range(1, SPAN + 1):
                lo = (SPAN - distance) * tok_rows
                kv_sent[distance - 1][m] = jnp.where(
                    hit,
                    kv_grad[lo : lo + tok_rows].astype(jnp.bfloat16),
                    kv_sent[distance - 1][m],
                )

    kv_out = jnp.stack(kv_total)
    for distance in range(1, SPAN + 1):
        returned = shifted(jnp.stack(kv_sent[distance - 1]), "ctx", -distance)
        kv_out = kv_out + returned.astype(jnp.float32)
    kv_out = kv_out.astype(jnp.bfloat16)
    gain_sum = butterfly_sum(gain_total, "ctx")
    return (
        jnp.stack([jnp.concatenate(parts) for parts in grad_stream])[None],
        kv_out[:, :, :kv_width][None],
        kv_out[:, :, kv_width:][None],
        gain_sum.reshape(1, feat_width),
    )


def solution(mesh):
    placed = (
        P(None, "ctx", None),
        P("pipe", None),
        P("pipe", None, "ctx", None),
        P("pipe", None, "ctx", None),
        P(),
        P(),
        P(None, "ctx"),
        P(),
    )
    return jax.shard_map(
        per_device,
        mesh=mesh,
        in_specs=placed,
        out_specs=(
            P("pipe", None, "ctx", None),
            P("pipe", None, "ctx", None),
            P("pipe", None, "ctx", None),
            P("pipe", None),
        ),
        check_vma=False,
    )
```

```python
import functools

import jax
import jax.numpy as jnp
from jax import lax
from jax.experimental import pallas as pl
from jax.sharding import PartitionSpec as P

HEAD_DIM = 128
SPAN = 2
CHUNKS = 1


NORM_EPS = 1e-05


def shifted(x, axis, by):
    size = lax.axis_size(axis)
    pairs = [(i, i + by) for i in range(size) if 0 <= i + by < size]
    return lax.ppermute(x, axis, pairs)


def butterfly_sum(x, axis):
    size = lax.axis_size(axis)
    if size & (size - 1):
        return lax.psum(x, axis)
    step = 1
    while step < size:
        pairs = [(i, i ^ step) for i in range(size)]
        x = x + lax.ppermute(x, axis, pairs)
        step *= 2
    return x

NT = (((1,), (1,)), ((), ()))
TN = (((0,), (0,)), ((), ()))

def fwd_kernel(q_ref, k_ref, v_ref, lo_ref, hi_ref, kp_ref, o_ref, lt_ref, *, heads, share, scale):
    rows = q_ref.shape[0]
    kpos = kp_ref[...]
    allowed = ((kpos >= lo_ref[...]) & (kpos <= hi_ref[...]))[None]
    for g in range(heads // share):
        gs = slice(g * HEAD_DIM, (g + 1) * HEAD_DIM)
        members = range(g * share, (g + 1) * share)
        q = jnp.concatenate([q_ref[:, h * HEAD_DIM : (h + 1) * HEAD_DIM] for h in members], axis=0)
        s = lax.dot_general(q, k_ref[:, gs], NT, preferred_element_type=jnp.float32) * scale
        s = s.reshape(share, rows, s.shape[-1])
        tot = jnp.sum(jnp.where(allowed, jnp.exp(s), 0.0), axis=2, keepdims=True)
        lt = jnp.log(tot)
        w = jnp.where(allowed, jnp.exp(s - lt), 0.0).astype(jnp.bfloat16)
        o = jnp.dot(w.reshape(share * rows, -1), v_ref[:, gs], preferred_element_type=jnp.float32)
        for j, h in enumerate(members):
            o_ref[:, h * HEAD_DIM : (h + 1) * HEAD_DIM] = o[j * rows : (j + 1) * rows].astype(o_ref.dtype)
            lt_ref[:, h : h + 1] = lt[j]

def bwd_kernel(q_ref, do_ref, att_ref, k_ref, v_ref, lt_ref, lo_ref, hi_ref, kp_ref, dq_ref, dk_ref, dv_ref, *, heads, share, scale):
    rows = q_ref.shape[0]
    kpos = kp_ref[...]
    allowed = ((kpos >= lo_ref[...]) & (kpos <= hi_ref[...]))[None]
    for g in range(heads // share):
        gs = slice(g * HEAD_DIM, (g + 1) * HEAD_DIM)
        members = range(g * share, (g + 1) * share)
        cols = [slice(h * HEAD_DIM, (h + 1) * HEAD_DIM) for h in members]
        q = jnp.concatenate([q_ref[:, c] for c in cols], axis=0)
        do = jnp.concatenate([do_ref[:, c] for c in cols], axis=0)
        att = jnp.concatenate([att_ref[:, c] for c in cols], axis=0)
        lt = jnp.stack([lt_ref[:, h : h + 1] for h in members])
        k = k_ref[:, gs]
        v = v_ref[:, gs]
        od = jnp.sum(do.astype(jnp.float32) * att.astype(jnp.float32), axis=1, keepdims=True)
        s = lax.dot_general(q, k, NT, preferred_element_type=jnp.float32) * scale
        s = s.reshape(share, rows, s.shape[-1])
        p = jnp.where(allowed, jnp.exp(s - lt), 0.0).reshape(share * rows, -1)
        dp = lax.dot_general(do, v, NT, preferred_element_type=jnp.float32)
        ds = (p * (dp - od) * scale).astype(jnp.bfloat16)
        w = p.astype(jnp.bfloat16)
        dq = jnp.dot(ds, k, preferred_element_type=jnp.float32)
        for j, c in enumerate(cols):
            dq_ref[:, c] = dq[j * rows : (j + 1) * rows]
        dk_ref[:, gs] = lax.dot_general(ds, q, TN, preferred_element_type=jnp.float32)
        dv_ref[:, gs] = lax.dot_general(w, do, TN, preferred_element_type=jnp.float32)

def attn_fwd(q, k, v, lo, hi, kp):
    rows, width = q.shape
    heads = width // HEAD_DIM
    share = heads // (k.shape[1] // HEAD_DIM)
    kern = functools.partial(fwd_kernel, heads=heads, share=share, scale=HEAD_DIM ** -0.5)
    return pl.pallas_call(kern, out_shape=(jax.ShapeDtypeStruct((rows, width), jnp.bfloat16), jax.ShapeDtypeStruct((rows, heads), jnp.float32)))(q, k, v, lo, hi, kp)

def attn_bwd(q, do, att, k, v, lt, lo, hi, kp):
    rows, width = q.shape
    heads = width // HEAD_DIM
    share = heads // (k.shape[1] // HEAD_DIM)
    kern = functools.partial(bwd_kernel, heads=heads, share=share, scale=HEAD_DIM ** -0.5)
    return pl.pallas_call(kern, out_shape=(jax.ShapeDtypeStruct((rows, width), jnp.float32), jax.ShapeDtypeStruct(k.shape, jnp.float32), jax.ShapeDtypeStruct(v.shape, jnp.float32)))(q, do, att, k, v, lt, lo, hi, kp)


def norm_rows(stream):
    values_f = stream.astype(jnp.float32)
    inv_rms = lax.rsqrt(jnp.mean(values_f * values_f, axis=-1) + NORM_EPS)
    return (values_f * inv_rms[:, None], inv_rms)


def per_device(hidden, gain, keys, values, cotangent, lengths, doc_start, block_mask):
    section = lax.axis_index("pipe")
    segment_count = lax.axis_size("pipe")
    index_of_block = lax.axis_index("ctx")
    micro_count, tok_rows, feat_width = hidden.shape
    kv_width = keys.shape[3]
    groups = kv_width // HEAD_DIM
    group_share = feat_width // HEAD_DIM // groups
    gain_row = gain[0]
    last_segment = segment_count - 1
    offsets = jnp.arange(tok_rows, dtype=jnp.int32)
    own_pos = index_of_block * tok_rows + offsets
    wide_rows = (SPAN + 1) * tok_rows
    key_pos = (index_of_block - SPAN) * tok_rows + jnp.arange(wide_rows, dtype=jnp.int32)
    time_steps = micro_count + segment_count - 1

    kv_own = jnp.concatenate([keys[0], values[0]], axis=-1)
    kv_wide = [
        jnp.concatenate(
            [shifted(kv_own[m], "ctx", distance) for distance in range(SPAN, 0, -1)] + [kv_own[m]]
        )
        for m in range(micro_count)
    ]
    key_wide = [kv_wide[m][:, :kv_width] for m in range(micro_count)]
    value_wide = [kv_wide[m][:, kv_width:] for m in range(micro_count)]
    lower_all = [doc_start[m][:, None] for m in range(micro_count)]
    upper = own_pos[:, None]
    key_row = key_pos[None, :]

    def pick(items, index):
        out = items[0]
        for m in range(1, len(items)):
            out = jnp.where(index == m, items[m], out)
        return out

    chunk_rows = tok_rows // CHUNKS
    cuts = [slice(c * chunk_rows, (c + 1) * chunk_rows) for c in range(CHUNKS)]
    received = [jnp.zeros((chunk_rows, feat_width), jnp.bfloat16) for _ in range(CHUNKS)]
    blank = lambda shape, kind: [[jnp.zeros(shape, kind) for _ in range(CHUNKS)] for _ in range(micro_count)]
    stream_store = blank((chunk_rows, feat_width), jnp.bfloat16)
    attended_store = blank((chunk_rows, feat_width), jnp.bfloat16)
    log_store = blank((chunk_rows, groups * group_share), jnp.float32)
    for time_step in range(time_steps):
        raw_index = time_step - section
        working_buffer = (raw_index >= 0) & (raw_index < micro_count)
        microbatch_index = jnp.clip(raw_index, 0, micro_count - 1)
        key_rows = pick(key_wide, microbatch_index)
        value_rows = pick(value_wide, microbatch_index)
        lower = pick(lower_all, microbatch_index)
        hidden_in = hidden[microbatch_index]
        for c, cut in enumerate(cuts):
            stream_in = jnp.where(section == 0, hidden_in[cut], received[c])
            normed, inv_rms = norm_rows(stream_in)
            queries = (normed * gain_row).astype(jnp.bfloat16)
            attended, log_total = attn_fwd(
                queries, key_rows, value_rows, lower[cut], upper[cut], key_row
            )
            stream_out = (stream_in.astype(jnp.float32) + attended.astype(jnp.float32)).astype(
                jnp.bfloat16
            )
            for m in range(micro_count):
                hit = working_buffer & (microbatch_index == m)
                stream_store[m][c] = jnp.where(hit, stream_in, stream_store[m][c])
                attended_store[m][c] = jnp.where(hit, attended, attended_store[m][c])
                log_store[m][c] = jnp.where(hit, log_total, log_store[m][c])
            if time_step < time_steps - 1:
                received[c] = shifted(stream_out, "pipe", 1)

    doc_ends = jnp.cumsum(lengths, axis=1)
    doc_starts = doc_ends - lengths
    seeds = []
    for m in range(micro_count):
        onehot = (
            (own_pos[:, None] >= doc_starts[m][None, :]) & (own_pos[:, None] < doc_ends[m][None, :])
        ).astype(jnp.float32)
        picked = jnp.dot(onehot, cotangent[m], precision=lax.Precision.HIGHEST)
        doc_length = jnp.dot(
            onehot, lengths[m].astype(jnp.float32), precision=lax.Precision.HIGHEST
        )
        seeds.append((picked / doc_length[:, None]).astype(jnp.bfloat16))

    received = [jnp.zeros((chunk_rows, feat_width), jnp.bfloat16) for _ in range(CHUNKS)]
    grad_stream = blank((chunk_rows, feat_width), jnp.bfloat16)
    kv_total = [jnp.zeros((tok_rows, 2 * kv_width), jnp.float32) for _ in range(micro_count)]
    kv_sent = [
        [jnp.zeros((tok_rows, 2 * kv_width), jnp.bfloat16) for _ in range(micro_count)]
        for _ in range(SPAN)
    ]
    gain_total = jnp.zeros((feat_width,), jnp.float32)
    for time_step in range(time_steps):
        raw_index = time_step - (last_segment - section)
        working_buffer = (raw_index >= 0) & (raw_index < micro_count)
        microbatch_index = jnp.clip(raw_index, 0, micro_count - 1)
        key_rows = pick(key_wide, microbatch_index)
        value_rows = pick(value_wide, microbatch_index)
        lower = pick(lower_all, microbatch_index)
        seed = pick(seeds, microbatch_index)
        kv_grad = None
        for c, cut in enumerate(cuts):
            out_grad = jnp.where(section == last_segment, seed[cut], received[c])
            stream_in = pick([stream_store[m][c] for m in range(micro_count)], microbatch_index)
            normed, inv_rms = norm_rows(stream_in)
            queries = (normed * gain_row).astype(jnp.bfloat16)
            query_grad, key_grad, value_grad = attn_bwd(
                queries,
                out_grad,
                pick([attended_store[m][c] for m in range(micro_count)], microbatch_index),
                key_rows,
                value_rows,
                pick([log_store[m][c] for m in range(micro_count)], microbatch_index),
                lower[cut],
                upper[cut],
                key_row,
            )
            part = jnp.concatenate([key_grad, value_grad], axis=-1)
            kv_grad = part if kv_grad is None else kv_grad + part
            gain_total = gain_total + jnp.where(
                working_buffer, jnp.sum(query_grad * normed, axis=0), 0.0
            )
            normed_grad = query_grad * gain_row
            norm_grad = inv_rms[:, None] * (
                normed_grad - normed * jnp.mean(normed_grad * normed, axis=-1, keepdims=True)
            )
            stream_grad = (out_grad.astype(jnp.float32) + norm_grad).astype(jnp.bfloat16)
            for m in range(micro_count):
                hit = working_buffer & (microbatch_index == m)
                grad_stream[m][c] = jnp.where(hit, stream_grad, grad_stream[m][c])
            if time_step < time_steps - 1:
                received[c] = shifted(stream_grad, "pipe", -1)
        for m in range(micro_count):
            hit = working_buffer & (microbatch_index == m)
            kv_total[m] = jnp.where(hit, kv_grad[SPAN * tok_rows :], kv_total[m])
            for distance in range(1, SPAN + 1):
                lo = (SPAN - distance) * tok_rows
                kv_sent[distance - 1][m] = jnp.where(
                    hit,
                    kv_grad[lo : lo + tok_rows].astype(jnp.bfloat16),
                    kv_sent[distance - 1][m],
                )

    kv_out = jnp.stack(kv_total)
    for distance in range(1, SPAN + 1):
        returned = shifted(jnp.stack(kv_sent[distance - 1]), "ctx", -distance)
        kv_out = kv_out + returned.astype(jnp.float32)
    kv_out = kv_out.astype(jnp.bfloat16)
    gain_sum = butterfly_sum(gain_total, "ctx")
    return (
        jnp.stack([jnp.concatenate(parts) for parts in grad_stream])[None],
        kv_out[:, :, :kv_width][None],
        kv_out[:, :, kv_width:][None],
        gain_sum.reshape(1, feat_width),
    )


def solution(mesh):
    placed = (
        P(None, "ctx", None),
        P("pipe", None),
        P("pipe", None, "ctx", None),
        P("pipe", None, "ctx", None),
        P(),
        P(),
        P(None, "ctx"),
        P(),
    )
    return jax.shard_map(
        per_device,
        mesh=mesh,
        in_specs=placed,
        out_specs=(
            P("pipe", None, "ctx", None),
            P("pipe", None, "ctx", None),
            P("pipe", None, "ctx", None),
            P("pipe", None),
        ),
        check_vma=False,
    )
```

```python
import functools

import jax
import jax.numpy as jnp
from jax import lax
from jax.experimental import pallas as pl
from jax.sharding import PartitionSpec as P

HEAD_DIM = 128
SPAN = 2
CHUNKS = 1


NORM_EPS = 1e-05


def shifted(x, axis, by):
    size = lax.axis_size(axis)
    pairs = [(i, i + by) for i in range(size) if 0 <= i + by < size]
    return lax.ppermute(x, axis, pairs)


def butterfly_sum(x, axis):
    size = lax.axis_size(axis)
    radices = []
    rest = size
    while rest % 4 == 0:
        radices.append(4)
        rest //= 4
    while rest % 2 == 0:
        radices.append(2)
        rest //= 2
    if rest != 1:
        return lax.psum(x, axis)
    me = lax.axis_index(axis)
    stride = 1
    for radix in radices:
        digit = (me // stride) % radix
        got = [x]
        for offset in range(1, radix):
            pairs = []
            for i in range(size):
                d = (i // stride) % radix
                pairs.append((i, i + (((d - offset) % radix) - d) * stride))
            got.append(lax.ppermute(x, axis, pairs))
        placed = []
        for a in range(radix):
            pick_a = got[0]
            for offset in range(1, radix):
                pick_a = jnp.where((a - digit) % radix == offset, got[offset], pick_a)
            placed.append(pick_a)
        while len(placed) > 1:
            placed = [placed[i] + placed[i + 1] for i in range(0, len(placed), 2)]
        x = placed[0]
        stride *= radix
    return x


NT = (((1,), (1,)), ((), ()))
TN = (((0,), (0,)), ((), ()))

def fwd_kernel(q_ref, k_ref, v_ref, lo_ref, hi_ref, kp_ref, o_ref, lt_ref, *, heads, share, scale):
    rows = q_ref.shape[0]
    kpos = kp_ref[...]
    allowed = ((kpos >= lo_ref[...]) & (kpos <= hi_ref[...]))[None]
    for g in range(heads // share):
        gs = slice(g * HEAD_DIM, (g + 1) * HEAD_DIM)
        members = range(g * share, (g + 1) * share)
        q = jnp.concatenate([q_ref[:, h * HEAD_DIM : (h + 1) * HEAD_DIM] for h in members], axis=0)
        s = lax.dot_general(q, k_ref[:, gs], NT, preferred_element_type=jnp.float32) * scale
        s = s.reshape(share, rows, s.shape[-1])
        tot = jnp.sum(jnp.where(allowed, jnp.exp(s), 0.0), axis=2, keepdims=True)
        lt = jnp.log(tot)
        w = jnp.where(allowed, jnp.exp(s - lt), 0.0).astype(jnp.bfloat16)
        o = jnp.dot(w.reshape(share * rows, -1), v_ref[:, gs], preferred_element_type=jnp.float32)
        for j, h in enumerate(members):
            o_ref[:, h * HEAD_DIM : (h + 1) * HEAD_DIM] = o[j * rows : (j + 1) * rows].astype(o_ref.dtype)
            lt_ref[:, h : h + 1] = lt[j]

def bwd_kernel(q_ref, do_ref, att_ref, k_ref, v_ref, lt_ref, lo_ref, hi_ref, kp_ref, dq_ref, dk_ref, dv_ref, *, heads, share, scale):
    rows = q_ref.shape[0]
    kpos = kp_ref[...]
    allowed = ((kpos >= lo_ref[...]) & (kpos <= hi_ref[...]))[None]
    for g in range(heads // share):
        gs = slice(g * HEAD_DIM, (g + 1) * HEAD_DIM)
        members = range(g * share, (g + 1) * share)
        cols = [slice(h * HEAD_DIM, (h + 1) * HEAD_DIM) for h in members]
        q = jnp.concatenate([q_ref[:, c] for c in cols], axis=0)
        do = jnp.concatenate([do_ref[:, c] for c in cols], axis=0)
        att = jnp.concatenate([att_ref[:, c] for c in cols], axis=0)
        lt = jnp.stack([lt_ref[:, h : h + 1] for h in members])
        k = k_ref[:, gs]
        v = v_ref[:, gs]
        od = jnp.sum(do.astype(jnp.float32) * att.astype(jnp.float32), axis=1, keepdims=True)
        s = lax.dot_general(q, k, NT, preferred_element_type=jnp.float32) * scale
        s = s.reshape(share, rows, s.shape[-1])
        p = jnp.where(allowed, jnp.exp(s - lt), 0.0).reshape(share * rows, -1)
        dp = lax.dot_general(do, v, NT, preferred_element_type=jnp.float32)
        ds = (p * (dp - od) * scale).astype(jnp.bfloat16)
        w = p.astype(jnp.bfloat16)
        dq = jnp.dot(ds, k, preferred_element_type=jnp.float32)
        for j, c in enumerate(cols):
            dq_ref[:, c] = dq[j * rows : (j + 1) * rows]
        dk_ref[:, gs] = lax.dot_general(ds, q, TN, preferred_element_type=jnp.float32)
        dv_ref[:, gs] = lax.dot_general(w, do, TN, preferred_element_type=jnp.float32)

def attn_fwd(q, k, v, lo, hi, kp):
    rows, width = q.shape
    heads = width // HEAD_DIM
    share = heads // (k.shape[1] // HEAD_DIM)
    kern = functools.partial(fwd_kernel, heads=heads, share=share, scale=HEAD_DIM ** -0.5)
    return pl.pallas_call(kern, out_shape=(jax.ShapeDtypeStruct((rows, width), jnp.bfloat16), jax.ShapeDtypeStruct((rows, heads), jnp.float32)))(q, k, v, lo, hi, kp)

def attn_bwd(q, do, att, k, v, lt, lo, hi, kp):
    rows, width = q.shape
    heads = width // HEAD_DIM
    share = heads // (k.shape[1] // HEAD_DIM)
    kern = functools.partial(bwd_kernel, heads=heads, share=share, scale=HEAD_DIM ** -0.5)
    return pl.pallas_call(kern, out_shape=(jax.ShapeDtypeStruct((rows, width), jnp.float32), jax.ShapeDtypeStruct(k.shape, jnp.float32), jax.ShapeDtypeStruct(v.shape, jnp.float32)))(q, do, att, k, v, lt, lo, hi, kp)


def norm_rows(stream):
    values_f = stream.astype(jnp.float32)
    inv_rms = lax.rsqrt(jnp.mean(values_f * values_f, axis=-1) + NORM_EPS)
    return (values_f * inv_rms[:, None], inv_rms)


def per_device(hidden, gain, keys, values, cotangent, lengths, doc_start, block_mask):
    section = lax.axis_index("pipe")
    segment_count = lax.axis_size("pipe")
    index_of_block = lax.axis_index("ctx")
    micro_count, tok_rows, feat_width = hidden.shape
    kv_width = keys.shape[3]
    groups = kv_width // HEAD_DIM
    group_share = feat_width // HEAD_DIM // groups
    gain_row = gain[0]
    last_segment = segment_count - 1
    offsets = jnp.arange(tok_rows, dtype=jnp.int32)
    own_pos = index_of_block * tok_rows + offsets
    wide_rows = (SPAN + 1) * tok_rows
    key_pos = (index_of_block - SPAN) * tok_rows + jnp.arange(wide_rows, dtype=jnp.int32)
    time_steps = micro_count + segment_count - 1

    kv_own = jnp.concatenate([keys[0], values[0]], axis=-1)
    kv_wide = [
        jnp.concatenate(
            [shifted(kv_own[m], "ctx", distance) for distance in range(SPAN, 0, -1)] + [kv_own[m]]
        )
        for m in range(micro_count)
    ]
    key_wide = [kv_wide[m][:, :kv_width] for m in range(micro_count)]
    value_wide = [kv_wide[m][:, kv_width:] for m in range(micro_count)]
    lower_all = [doc_start[m][:, None] for m in range(micro_count)]
    upper = own_pos[:, None]
    key_row = key_pos[None, :]

    def pick(items, index):
        out = items[0]
        for m in range(1, len(items)):
            out = jnp.where(index == m, items[m], out)
        return out

    chunk_rows = tok_rows // CHUNKS
    cuts = [slice(c * chunk_rows, (c + 1) * chunk_rows) for c in range(CHUNKS)]
    received = [jnp.zeros((chunk_rows, feat_width), jnp.bfloat16) for _ in range(CHUNKS)]
    blank = lambda shape, kind: [[jnp.zeros(shape, kind) for _ in range(CHUNKS)] for _ in range(micro_count)]
    stream_store = blank((chunk_rows, feat_width), jnp.bfloat16)
    attended_store = blank((chunk_rows, feat_width), jnp.bfloat16)
    log_store = blank((chunk_rows, groups * group_share), jnp.float32)
    for time_step in range(time_steps):
        raw_index = time_step - section
        working_buffer = (raw_index >= 0) & (raw_index < micro_count)
        microbatch_index = jnp.clip(raw_index, 0, micro_count - 1)
        key_rows = pick(key_wide, microbatch_index)
        value_rows = pick(value_wide, microbatch_index)
        lower = pick(lower_all, microbatch_index)
        hidden_in = hidden[microbatch_index]
        for c, cut in enumerate(cuts):
            stream_in = jnp.where(section == 0, hidden_in[cut], received[c])
            normed, inv_rms = norm_rows(stream_in)
            queries = (normed * gain_row).astype(jnp.bfloat16)
            attended, log_total = attn_fwd(
                queries, key_rows, value_rows, lower[cut], upper[cut], key_row
            )
            stream_out = (stream_in.astype(jnp.float32) + attended.astype(jnp.float32)).astype(
                jnp.bfloat16
            )
            for m in range(micro_count):
                hit = working_buffer & (microbatch_index == m)
                stream_store[m][c] = jnp.where(hit, stream_in, stream_store[m][c])
                attended_store[m][c] = jnp.where(hit, attended, attended_store[m][c])
                log_store[m][c] = jnp.where(hit, log_total, log_store[m][c])
            if time_step < time_steps - 1:
                received[c] = shifted(stream_out, "pipe", 1)

    doc_ends = jnp.cumsum(lengths, axis=1)
    doc_starts = doc_ends - lengths
    seeds = []
    for m in range(micro_count):
        onehot = (
            (own_pos[:, None] >= doc_starts[m][None, :]) & (own_pos[:, None] < doc_ends[m][None, :])
        ).astype(jnp.float32)
        picked = jnp.dot(onehot, cotangent[m], precision=lax.Precision.HIGHEST)
        doc_length = jnp.dot(
            onehot, lengths[m].astype(jnp.float32), precision=lax.Precision.HIGHEST
        )
        seeds.append((picked / doc_length[:, None]).astype(jnp.bfloat16))

    received = [jnp.zeros((chunk_rows, feat_width), jnp.bfloat16) for _ in range(CHUNKS)]
    grad_stream = blank((chunk_rows, feat_width), jnp.bfloat16)
    kv_total = [jnp.zeros((tok_rows, 2 * kv_width), jnp.float32) for _ in range(micro_count)]
    kv_sent = [
        [jnp.zeros((tok_rows, 2 * kv_width), jnp.bfloat16) for _ in range(micro_count)]
        for _ in range(SPAN)
    ]
    gain_total = jnp.zeros((feat_width,), jnp.float32)
    returned_kv = [jnp.zeros((tok_rows, 2 * kv_width), jnp.float32) for _ in range(micro_count)]
    for time_step in range(time_steps):
        raw_index = time_step - (last_segment - section)
        working_buffer = (raw_index >= 0) & (raw_index < micro_count)
        microbatch_index = jnp.clip(raw_index, 0, micro_count - 1)
        key_rows = pick(key_wide, microbatch_index)
        value_rows = pick(value_wide, microbatch_index)
        lower = pick(lower_all, microbatch_index)
        seed = pick(seeds, microbatch_index)
        kv_grad = None
        for c, cut in enumerate(cuts):
            out_grad = jnp.where(section == last_segment, seed[cut], received[c])
            stream_in = pick([stream_store[m][c] for m in range(micro_count)], microbatch_index)
            normed, inv_rms = norm_rows(stream_in)
            queries = (normed * gain_row).astype(jnp.bfloat16)
            query_grad, key_grad, value_grad = attn_bwd(
                queries,
                out_grad,
                pick([attended_store[m][c] for m in range(micro_count)], microbatch_index),
                key_rows,
                value_rows,
                pick([log_store[m][c] for m in range(micro_count)], microbatch_index),
                lower[cut],
                upper[cut],
                key_row,
            )
            part = jnp.concatenate([key_grad, value_grad], axis=-1)
            kv_grad = part if kv_grad is None else kv_grad + part
            gain_total = gain_total + jnp.where(
                working_buffer, jnp.sum(query_grad * normed, axis=0), 0.0
            )
            normed_grad = query_grad * gain_row
            norm_grad = inv_rms[:, None] * (
                normed_grad - normed * jnp.mean(normed_grad * normed, axis=-1, keepdims=True)
            )
            stream_grad = (out_grad.astype(jnp.float32) + norm_grad).astype(jnp.bfloat16)
            for m in range(micro_count):
                hit = working_buffer & (microbatch_index == m)
                grad_stream[m][c] = jnp.where(hit, stream_grad, grad_stream[m][c])
            if time_step < time_steps - 1:
                received[c] = shifted(stream_grad, "pipe", -1)
        for m in range(micro_count):
            hit = working_buffer & (microbatch_index == m)
            kv_total[m] = jnp.where(hit, kv_grad[SPAN * tok_rows :], kv_total[m])
            for distance in range(1, SPAN + 1):
                lo = (SPAN - distance) * tok_rows
                kv_sent[distance - 1][m] = jnp.where(
                    hit,
                    kv_grad[lo : lo + tok_rows].astype(jnp.bfloat16),
                    kv_sent[distance - 1][m],
                )
        for m in range(micro_count):
            if time_step == m + segment_count - 1:
                for distance in range(1, SPAN + 1):
                    returned = shifted(kv_sent[distance - 1][m], "ctx", -distance)
                    returned_kv[m] = returned_kv[m] + returned.astype(jnp.float32)

    kv_out = jnp.stack(
        [kv_total[m] + returned_kv[m] for m in range(micro_count)]
    ).astype(jnp.bfloat16)
    gain_sum = butterfly_sum(gain_total, "ctx")
    return (
        jnp.stack([jnp.concatenate(parts) for parts in grad_stream])[None],
        kv_out[:, :, :kv_width][None],
        kv_out[:, :, kv_width:][None],
        gain_sum.reshape(1, feat_width),
    )


def solution(mesh):
    placed = (
        P(None, "ctx", None),
        P("pipe", None),
        P("pipe", None, "ctx", None),
        P("pipe", None, "ctx", None),
        P(),
        P(),
        P(None, "ctx"),
        P(),
    )
    return jax.shard_map(
        per_device,
        mesh=mesh,
        in_specs=placed,
        out_specs=(
            P("pipe", None, "ctx", None),
            P("pipe", None, "ctx", None),
            P("pipe", None, "ctx", None),
            P("pipe", None),
        ),
        check_vma=False,
    )
```

```python
import functools

import jax
import jax.numpy as jnp
from jax import lax
from jax.experimental import pallas as pl
from jax.experimental.pallas import tpu as pltpu
from jax.sharding import PartitionSpec as P

HEAD_DIM = 128
SPAN = 2
CHUNKS = 1


NORM_EPS = 1e-05


def shifted(x, axis, by):
    size = lax.axis_size(axis)
    pairs = [(i, i + by) for i in range(size) if 0 <= i + by < size]
    return lax.ppermute(x, axis, pairs)


def butterfly_sum(x, axis):
    size = lax.axis_size(axis)
    radices = []
    rest = size
    while rest % 4 == 0:
        radices.append(4)
        rest //= 4
    while rest % 2 == 0:
        radices.append(2)
        rest //= 2
    if rest != 1:
        return lax.psum(x, axis)
    me = lax.axis_index(axis)
    stride = 1
    for radix in radices:
        digit = (me // stride) % radix
        got = [x]
        for offset in range(1, radix):
            pairs = []
            for i in range(size):
                d = (i // stride) % radix
                pairs.append((i, i + (((d - offset) % radix) - d) * stride))
            got.append(lax.ppermute(x, axis, pairs))
        placed = []
        for a in range(radix):
            pick_a = got[0]
            for offset in range(1, radix):
                pick_a = jnp.where((a - digit) % radix == offset, got[offset], pick_a)
            placed.append(pick_a)
        while len(placed) > 1:
            placed = [placed[i] + placed[i + 1] for i in range(0, len(placed), 2)]
        x = placed[0]
        stride *= radix
    return x


NT = (((1,), (1,)), ((), ()))
TN = (((0,), (0,)), ((), ()))

def norm_in_kernel(stream_ref, gain_ref):
    values_f = stream_ref[...].astype(jnp.float32)
    inv_rms = lax.rsqrt(jnp.mean(values_f * values_f, axis=1, keepdims=True) + NORM_EPS)
    normed = values_f * inv_rms
    return values_f, inv_rms, normed, (normed * gain_ref[...]).astype(jnp.bfloat16)


def fwd_kernel(x_ref, gain_ref, k_ref, v_ref, lo_ref, hi_ref, kp_ref, out_ref, o_ref, lt_ref, *, heads, share, scale):
    values_f, _, _, queries = norm_in_kernel(x_ref, gain_ref)
    rows = x_ref.shape[0]
    kpos = kp_ref[...]
    allowed = ((kpos >= lo_ref[...]) & (kpos <= hi_ref[...]))[None]
    for g in range(heads // share):
        gs = slice(g * HEAD_DIM, (g + 1) * HEAD_DIM)
        members = range(g * share, (g + 1) * share)
        q = jnp.concatenate([queries[:, h * HEAD_DIM : (h + 1) * HEAD_DIM] for h in members], axis=0)
        s = lax.dot_general(q, k_ref[:, gs], NT, preferred_element_type=jnp.float32) * scale
        s = s.reshape(share, rows, s.shape[-1])
        tot = jnp.sum(jnp.where(allowed, jnp.exp(s), 0.0), axis=2, keepdims=True)
        lt = jnp.log(tot)
        w = jnp.where(allowed, jnp.exp(s - lt), 0.0).astype(jnp.bfloat16)
        o = jnp.dot(w.reshape(share * rows, -1), v_ref[:, gs], preferred_element_type=jnp.float32)
        for j, h in enumerate(members):
            hs = slice(h * HEAD_DIM, (h + 1) * HEAD_DIM)
            att = o[j * rows : (j + 1) * rows].astype(jnp.bfloat16)
            o_ref[:, hs] = att
            out_ref[:, hs] = (values_f[:, hs] + att.astype(jnp.float32)).astype(out_ref.dtype)
            lt_ref[:, h : h + 1] = lt[j]


def bwd_kernel(x_ref, gain_ref, do_ref, att_ref, k_ref, v_ref, lt_ref, lo_ref, hi_ref, kp_ref, sg_ref, gp_ref, dk_ref, dv_ref, dq_ref, *, heads, share, scale):
    _, inv_rms, normed, queries = norm_in_kernel(x_ref, gain_ref)
    rows = x_ref.shape[0]
    kpos = kp_ref[...]
    allowed = ((kpos >= lo_ref[...]) & (kpos <= hi_ref[...]))[None]
    for g in range(heads // share):
        gs = slice(g * HEAD_DIM, (g + 1) * HEAD_DIM)
        members = range(g * share, (g + 1) * share)
        cols = [slice(h * HEAD_DIM, (h + 1) * HEAD_DIM) for h in members]
        q = jnp.concatenate([queries[:, c] for c in cols], axis=0)
        do = jnp.concatenate([do_ref[:, c] for c in cols], axis=0)
        att = jnp.concatenate([att_ref[:, c] for c in cols], axis=0)
        lt = jnp.stack([lt_ref[:, h : h + 1] for h in members])
        k = k_ref[:, gs]
        v = v_ref[:, gs]
        od = jnp.sum(do.astype(jnp.float32) * att.astype(jnp.float32), axis=1, keepdims=True)
        s = lax.dot_general(q, k, NT, preferred_element_type=jnp.float32) * scale
        s = s.reshape(share, rows, s.shape[-1])
        p = jnp.where(allowed, jnp.exp(s - lt), 0.0).reshape(share * rows, -1)
        dp = lax.dot_general(do, v, NT, preferred_element_type=jnp.float32)
        ds = (p * (dp - od) * scale).astype(jnp.bfloat16)
        w = p.astype(jnp.bfloat16)
        dq = jnp.dot(ds, k, preferred_element_type=jnp.float32)
        for j, c in enumerate(cols):
            dq_ref[:, c] = dq[j * rows : (j + 1) * rows]
        dk_ref[:, gs] = lax.dot_general(ds, q, TN, preferred_element_type=jnp.float32)
        dv_ref[:, gs] = lax.dot_general(w, do, TN, preferred_element_type=jnp.float32)
    query_grad = dq_ref[...]
    gp_ref[...] = jnp.sum(query_grad * normed, axis=0, keepdims=True)
    normed_grad = query_grad * gain_ref[...]
    norm_grad = inv_rms * (
        normed_grad - normed * jnp.mean(normed_grad * normed, axis=1, keepdims=True)
    )
    sg_ref[...] = (do_ref[...].astype(jnp.float32) + norm_grad).astype(sg_ref.dtype)


def attn_fwd(x, gain, k, v, lo, hi, kp):
    rows, width = x.shape
    heads = width // HEAD_DIM
    share = heads // (k.shape[1] // HEAD_DIM)
    kern = functools.partial(fwd_kernel, heads=heads, share=share, scale=HEAD_DIM ** -0.5)
    return pl.pallas_call(
        kern,
        out_shape=(
            jax.ShapeDtypeStruct((rows, width), jnp.bfloat16),
            jax.ShapeDtypeStruct((rows, width), jnp.bfloat16),
            jax.ShapeDtypeStruct((rows, heads), jnp.float32),
        ),
    )(x, gain, k, v, lo, hi, kp)


def attn_bwd(x, gain, do, att, k, v, lt, lo, hi, kp):
    rows, width = x.shape
    heads = width // HEAD_DIM
    share = heads // (k.shape[1] // HEAD_DIM)
    kern = functools.partial(bwd_kernel, heads=heads, share=share, scale=HEAD_DIM ** -0.5)
    sg, gp, dk, dv = pl.pallas_call(
        kern,
        out_shape=(
            jax.ShapeDtypeStruct((rows, width), jnp.bfloat16),
            jax.ShapeDtypeStruct((1, width), jnp.float32),
            jax.ShapeDtypeStruct(k.shape, jnp.float32),
            jax.ShapeDtypeStruct(v.shape, jnp.float32),
        ),
        scratch_shapes=[pltpu.VMEM((rows, width), jnp.float32)],
    )(x, gain, do, att, k, v, lt, lo, hi, kp)
    return sg, gp[0], dk, dv


def per_device(hidden, gain, keys, values, cotangent, lengths, doc_start, block_mask):
    section = lax.axis_index("pipe")
    segment_count = lax.axis_size("pipe")
    index_of_block = lax.axis_index("ctx")
    micro_count, tok_rows, feat_width = hidden.shape
    kv_width = keys.shape[3]
    groups = kv_width // HEAD_DIM
    group_share = feat_width // HEAD_DIM // groups
    gain_row = gain[0]
    last_segment = segment_count - 1
    offsets = jnp.arange(tok_rows, dtype=jnp.int32)
    own_pos = index_of_block * tok_rows + offsets
    wide_rows = (SPAN + 1) * tok_rows
    key_pos = (index_of_block - SPAN) * tok_rows + jnp.arange(wide_rows, dtype=jnp.int32)
    time_steps = micro_count + segment_count - 1

    kv_own = jnp.concatenate([keys[0], values[0]], axis=-1)
    kv_wide = [
        jnp.concatenate(
            [shifted(kv_own[m], "ctx", distance) for distance in range(SPAN, 0, -1)] + [kv_own[m]]
        )
        for m in range(micro_count)
    ]
    key_wide = [kv_wide[m][:, :kv_width] for m in range(micro_count)]
    value_wide = [kv_wide[m][:, kv_width:] for m in range(micro_count)]
    lower_all = [doc_start[m][:, None] for m in range(micro_count)]
    upper = own_pos[:, None]
    key_row = key_pos[None, :]

    def pick(items, index):
        out = items[0]
        for m in range(1, len(items)):
            out = jnp.where(index == m, items[m], out)
        return out

    chunk_rows = tok_rows // CHUNKS
    cuts = [slice(c * chunk_rows, (c + 1) * chunk_rows) for c in range(CHUNKS)]
    received = [jnp.zeros((chunk_rows, feat_width), jnp.bfloat16) for _ in range(CHUNKS)]
    blank = lambda shape, kind: [[jnp.zeros(shape, kind) for _ in range(CHUNKS)] for _ in range(micro_count)]
    stream_store = blank((chunk_rows, feat_width), jnp.bfloat16)
    attended_store = blank((chunk_rows, feat_width), jnp.bfloat16)
    log_store = blank((chunk_rows, groups * group_share), jnp.float32)
    for time_step in range(time_steps):
        raw_index = time_step - section
        working_buffer = (raw_index >= 0) & (raw_index < micro_count)
        microbatch_index = jnp.clip(raw_index, 0, micro_count - 1)
        key_rows = pick(key_wide, microbatch_index)
        value_rows = pick(value_wide, microbatch_index)
        lower = pick(lower_all, microbatch_index)
        hidden_in = hidden[microbatch_index]
        for c, cut in enumerate(cuts):
            stream_in = jnp.where(section == 0, hidden_in[cut], received[c])
            stream_out, attended, log_total = attn_fwd(
                stream_in, gain_row[None], key_rows, value_rows, lower[cut], upper[cut], key_row
            )
            for m in range(micro_count):
                hit = working_buffer & (microbatch_index == m)
                stream_store[m][c] = jnp.where(hit, stream_in, stream_store[m][c])
                attended_store[m][c] = jnp.where(hit, attended, attended_store[m][c])
                log_store[m][c] = jnp.where(hit, log_total, log_store[m][c])
            if time_step < time_steps - 1:
                received[c] = shifted(stream_out, "pipe", 1)

    doc_ends = jnp.cumsum(lengths, axis=1)
    doc_starts = doc_ends - lengths
    seeds = []
    for m in range(micro_count):
        onehot = (
            (own_pos[:, None] >= doc_starts[m][None, :]) & (own_pos[:, None] < doc_ends[m][None, :])
        ).astype(jnp.float32)
        picked = jnp.dot(onehot, cotangent[m], precision=lax.Precision.HIGHEST)
        doc_length = jnp.dot(
            onehot, lengths[m].astype(jnp.float32), precision=lax.Precision.HIGHEST
        )
        seeds.append((picked / doc_length[:, None]).astype(jnp.bfloat16))

    received = [jnp.zeros((chunk_rows, feat_width), jnp.bfloat16) for _ in range(CHUNKS)]
    grad_stream = blank((chunk_rows, feat_width), jnp.bfloat16)
    kv_total = [jnp.zeros((tok_rows, 2 * kv_width), jnp.float32) for _ in range(micro_count)]
    kv_sent = [
        [jnp.zeros((tok_rows, 2 * kv_width), jnp.bfloat16) for _ in range(micro_count)]
        for _ in range(SPAN)
    ]
    gain_total = jnp.zeros((feat_width,), jnp.float32)
    returned_kv = [jnp.zeros((tok_rows, 2 * kv_width), jnp.float32) for _ in range(micro_count)]
    for time_step in range(time_steps):
        raw_index = time_step - (last_segment - section)
        working_buffer = (raw_index >= 0) & (raw_index < micro_count)
        microbatch_index = jnp.clip(raw_index, 0, micro_count - 1)
        key_rows = pick(key_wide, microbatch_index)
        value_rows = pick(value_wide, microbatch_index)
        lower = pick(lower_all, microbatch_index)
        seed = pick(seeds, microbatch_index)
        kv_grad = None
        for c, cut in enumerate(cuts):
            out_grad = jnp.where(section == last_segment, seed[cut], received[c])
            stream_in = pick([stream_store[m][c] for m in range(micro_count)], microbatch_index)
            stream_grad, gain_part, key_grad, value_grad = attn_bwd(
                stream_in,
                gain_row[None],
                out_grad,
                pick([attended_store[m][c] for m in range(micro_count)], microbatch_index),
                key_rows,
                value_rows,
                pick([log_store[m][c] for m in range(micro_count)], microbatch_index),
                lower[cut],
                upper[cut],
                key_row,
            )
            part = jnp.concatenate([key_grad, value_grad], axis=-1)
            kv_grad = part if kv_grad is None else kv_grad + part
            gain_total = gain_total + jnp.where(working_buffer, gain_part, 0.0)
            for m in range(micro_count):
                hit = working_buffer & (microbatch_index == m)
                grad_stream[m][c] = jnp.where(hit, stream_grad, grad_stream[m][c])
            if time_step < time_steps - 1:
                received[c] = shifted(stream_grad, "pipe", -1)
        for m in range(micro_count):
            hit = working_buffer & (microbatch_index == m)
            kv_total[m] = jnp.where(hit, kv_grad[SPAN * tok_rows :], kv_total[m])
            for distance in range(1, SPAN + 1):
                lo = (SPAN - distance) * tok_rows
                kv_sent[distance - 1][m] = jnp.where(
                    hit,
                    kv_grad[lo : lo + tok_rows].astype(jnp.bfloat16),
                    kv_sent[distance - 1][m],
                )
        for m in range(micro_count):
            if time_step == m + segment_count - 1:
                for distance in range(1, SPAN + 1):
                    returned = shifted(kv_sent[distance - 1][m], "ctx", -distance)
                    returned_kv[m] = returned_kv[m] + returned.astype(jnp.float32)

    kv_out = jnp.stack(
        [kv_total[m] + returned_kv[m] for m in range(micro_count)]
    ).astype(jnp.bfloat16)
    gain_sum = butterfly_sum(gain_total, "ctx")
    return (
        jnp.stack([jnp.concatenate(parts) for parts in grad_stream])[None],
        kv_out[:, :, :kv_width][None],
        kv_out[:, :, kv_width:][None],
        gain_sum.reshape(1, feat_width),
    )


def solution(mesh):
    placed = (
        P(None, "ctx", None),
        P("pipe", None),
        P("pipe", None, "ctx", None),
        P("pipe", None, "ctx", None),
        P(),
        P(),
        P(None, "ctx"),
        P(),
    )
    return jax.shard_map(
        per_device,
        mesh=mesh,
        in_specs=placed,
        out_specs=(
            P("pipe", None, "ctx", None),
            P("pipe", None, "ctx", None),
            P("pipe", None, "ctx", None),
            P("pipe", None),
        ),
        check_vma=False,
    )
```

```python
import functools

import jax
import jax.numpy as jnp
from jax import lax
from jax.experimental import pallas as pl
from jax.experimental.pallas import tpu as pltpu
from jax.sharding import PartitionSpec as P

HEAD_DIM = 128
SPAN = 2
CHUNKS = 1


NORM_EPS = 1e-05


def shifted(x, axis, by):
    size = lax.axis_size(axis)
    pairs = [(i, i + by) for i in range(size) if 0 <= i + by < size]
    return lax.ppermute(x, axis, pairs)


def butterfly_sum(x, axis):
    size = lax.axis_size(axis)
    radices = []
    rest = size
    while rest % 4 == 0:
        radices.append(4)
        rest //= 4
    while rest % 2 == 0:
        radices.append(2)
        rest //= 2
    if rest != 1:
        return lax.psum(x, axis)
    me = lax.axis_index(axis)
    stride = 1
    for radix in radices:
        digit = (me // stride) % radix
        got = [x]
        for offset in range(1, radix):
            pairs = []
            for i in range(size):
                d = (i // stride) % radix
                pairs.append((i, i + (((d - offset) % radix) - d) * stride))
            got.append(lax.ppermute(x, axis, pairs))
        placed = []
        for a in range(radix):
            pick_a = got[0]
            for offset in range(1, radix):
                pick_a = jnp.where((a - digit) % radix == offset, got[offset], pick_a)
            placed.append(pick_a)
        while len(placed) > 1:
            placed = [placed[i] + placed[i + 1] for i in range(0, len(placed), 2)]
        x = placed[0]
        stride *= radix
    return x


NT = (((1,), (1,)), ((), ()))
TN = (((0,), (0,)), ((), ()))

def norm_in_kernel(stream_ref, gain_ref):
    values_f = stream_ref[...].astype(jnp.float32)
    inv_rms = lax.rsqrt(jnp.mean(values_f * values_f, axis=1, keepdims=True) + NORM_EPS)
    normed = values_f * inv_rms
    return values_f, inv_rms, normed, (normed * gain_ref[...]).astype(jnp.bfloat16)


def fwd_kernel(x_ref, gain_ref, k_ref, v_ref, lo_ref, hi_ref, kp_ref, out_ref, o_ref, lt_ref, *, heads, share, scale):
    values_f, _, _, queries = norm_in_kernel(x_ref, gain_ref)
    rows = x_ref.shape[0]
    kpos = kp_ref[...]
    allowed = ((kpos >= lo_ref[...]) & (kpos <= hi_ref[...]))[None]
    for g in range(heads // share):
        gs = slice(g * HEAD_DIM, (g + 1) * HEAD_DIM)
        members = range(g * share, (g + 1) * share)
        q = jnp.concatenate([queries[:, h * HEAD_DIM : (h + 1) * HEAD_DIM] for h in members], axis=0)
        s = lax.dot_general(q, k_ref[:, gs], NT, preferred_element_type=jnp.float32) * scale
        s = s.reshape(share, rows, s.shape[-1])
        tot = jnp.sum(jnp.where(allowed, jnp.exp(s), 0.0), axis=2, keepdims=True)
        lt = jnp.log(tot)
        w = jnp.where(allowed, jnp.exp(s - lt), 0.0).astype(jnp.bfloat16)
        o = jnp.dot(w.reshape(share * rows, -1), v_ref[:, gs], preferred_element_type=jnp.float32)
        for j, h in enumerate(members):
            hs = slice(h * HEAD_DIM, (h + 1) * HEAD_DIM)
            att = o[j * rows : (j + 1) * rows].astype(jnp.bfloat16)
            o_ref[:, hs] = att
            out_ref[:, hs] = (values_f[:, hs] + att.astype(jnp.float32)).astype(out_ref.dtype)
            lt_ref[:, h : h + 1] = lt[j]


def bwd_kernel(x_ref, gain_ref, do_ref, att_ref, k_ref, v_ref, lt_ref, lo_ref, hi_ref, kp_ref, sg_ref, gp_ref, dk_ref, dv_ref, dq_ref, *, heads, share, scale):
    _, inv_rms, normed, queries = norm_in_kernel(x_ref, gain_ref)
    rows = x_ref.shape[0]
    kpos = kp_ref[...]
    allowed = ((kpos >= lo_ref[...]) & (kpos <= hi_ref[...]))[None]
    for g in range(heads // share):
        gs = slice(g * HEAD_DIM, (g + 1) * HEAD_DIM)
        members = range(g * share, (g + 1) * share)
        cols = [slice(h * HEAD_DIM, (h + 1) * HEAD_DIM) for h in members]
        q = jnp.concatenate([queries[:, c] for c in cols], axis=0)
        do = jnp.concatenate([do_ref[:, c] for c in cols], axis=0)
        att = jnp.concatenate([att_ref[:, c] for c in cols], axis=0)
        lt = jnp.stack([lt_ref[:, h : h + 1] for h in members])
        k = k_ref[:, gs]
        v = v_ref[:, gs]
        od = jnp.sum(do.astype(jnp.float32) * att.astype(jnp.float32), axis=1, keepdims=True)
        s = lax.dot_general(q, k, NT, preferred_element_type=jnp.float32) * scale
        s = s.reshape(share, rows, s.shape[-1])
        p = jnp.where(allowed, jnp.exp(s - lt), 0.0).reshape(share * rows, -1)
        dp = lax.dot_general(do, v, NT, preferred_element_type=jnp.float32)
        ds = (p * (dp - od) * scale).astype(jnp.bfloat16)
        w = p.astype(jnp.bfloat16)
        dq = jnp.dot(ds, k, preferred_element_type=jnp.float32)
        for j, c in enumerate(cols):
            dq_ref[:, c] = dq[j * rows : (j + 1) * rows]
        dk_ref[:, gs] = lax.dot_general(ds, q, TN, preferred_element_type=jnp.float32)
        dv_ref[:, gs] = lax.dot_general(w, do, TN, preferred_element_type=jnp.float32)
    query_grad = dq_ref[...]
    gp_ref[...] = jnp.sum(query_grad * normed, axis=0, keepdims=True)
    normed_grad = query_grad * gain_ref[...]
    norm_grad = inv_rms * (
        normed_grad - normed * jnp.mean(normed_grad * normed, axis=1, keepdims=True)
    )
    sg_ref[...] = (do_ref[...].astype(jnp.float32) + norm_grad).astype(sg_ref.dtype)


def attn_fwd(x, gain, k, v, lo, hi, kp):
    rows, width = x.shape
    heads = width // HEAD_DIM
    share = heads // (k.shape[1] // HEAD_DIM)
    kern = functools.partial(fwd_kernel, heads=heads, share=share, scale=HEAD_DIM ** -0.5)
    return pl.pallas_call(
        kern,
        out_shape=(
            jax.ShapeDtypeStruct((rows, width), jnp.bfloat16),
            jax.ShapeDtypeStruct((rows, width), jnp.bfloat16),
            jax.ShapeDtypeStruct((rows, heads), jnp.float32),
        ),
    )(x, gain, k, v, lo, hi, kp)


def attn_bwd(x, gain, do, att, k, v, lt, lo, hi, kp):
    rows, width = x.shape
    heads = width // HEAD_DIM
    share = heads // (k.shape[1] // HEAD_DIM)
    kern = functools.partial(bwd_kernel, heads=heads, share=share, scale=HEAD_DIM ** -0.5)
    sg, gp, dk, dv = pl.pallas_call(
        kern,
        out_shape=(
            jax.ShapeDtypeStruct((rows, width), jnp.bfloat16),
            jax.ShapeDtypeStruct((1, width), jnp.float32),
            jax.ShapeDtypeStruct(k.shape, jnp.float32),
            jax.ShapeDtypeStruct(v.shape, jnp.float32),
        ),
        scratch_shapes=[pltpu.VMEM((rows, width), jnp.float32)],
    )(x, gain, do, att, k, v, lt, lo, hi, kp)
    return sg, gp[0], dk, dv


def per_device(hidden, gain, keys, values, cotangent, lengths, doc_start, block_mask):
    section = lax.axis_index("pipe")
    segment_count = lax.axis_size("pipe")
    index_of_block = lax.axis_index("ctx")
    micro_count, tok_rows, feat_width = hidden.shape
    kv_width = keys.shape[3]
    groups = kv_width // HEAD_DIM
    group_share = feat_width // HEAD_DIM // groups
    gain_row = gain[0]
    last_segment = segment_count - 1
    offsets = jnp.arange(tok_rows, dtype=jnp.int32)
    own_pos = index_of_block * tok_rows + offsets
    wide_rows = (SPAN + 1) * tok_rows
    key_pos = (index_of_block - SPAN) * tok_rows + jnp.arange(wide_rows, dtype=jnp.int32)
    time_steps = micro_count + segment_count - 1

    kv_own = jnp.concatenate([keys[0], values[0]], axis=-1)
    def window_of(own):
        return jnp.concatenate(
            [shifted(own, "ctx", distance) for distance in range(SPAN, 0, -1)] + [own]
        )

    kv_wide = [window_of(kv_own[0])] + [None] * (micro_count - 1)
    lower_all = [doc_start[m][:, None] for m in range(micro_count)]
    upper = own_pos[:, None]
    key_row = key_pos[None, :]

    def pick(items, index):
        out = items[0]
        for m in range(1, len(items)):
            out = jnp.where(index == m, items[m], out)
        return out

    slots = micro_count + 1
    received = jnp.zeros((tok_rows, feat_width), jnp.bfloat16)
    stream_store = jnp.zeros((slots, tok_rows, feat_width), jnp.bfloat16)
    attended_store = jnp.zeros((slots, tok_rows, feat_width), jnp.bfloat16)
    log_store = jnp.zeros((slots, tok_rows, groups * group_share), jnp.float32)
    for time_step in range(time_steps):
        raw_index = time_step - section
        working_buffer = (raw_index >= 0) & (raw_index < micro_count)
        microbatch_index = jnp.clip(raw_index, 0, micro_count - 1)
        slot = jnp.where(working_buffer, microbatch_index, micro_count)
        ready = [m for m in range(micro_count) if kv_wide[m] is not None]
        window = pick([kv_wide[m] for m in ready], jnp.minimum(microbatch_index, len(ready) - 1))
        stream_in = jnp.where(section == 0, hidden[microbatch_index], received)
        stream_out, attended, log_total = attn_fwd(
            stream_in,
            gain_row[None],
            window[:, :kv_width],
            window[:, kv_width:],
            pick(lower_all, microbatch_index),
            upper,
            key_row,
        )
        for m in range(micro_count):
            if kv_wide[m] is None and m == time_step + 1:
                tied, _ = lax.optimization_barrier((kv_own[m], attended))
                kv_wide[m] = window_of(tied)
        stream_store = lax.dynamic_update_index_in_dim(stream_store, stream_in, slot, 0)
        attended_store = lax.dynamic_update_index_in_dim(attended_store, attended, slot, 0)
        log_store = lax.dynamic_update_index_in_dim(log_store, log_total, slot, 0)
        if time_step < time_steps - 1:
            received = shifted(stream_out, "pipe", 1)
    key_wide = [kv_wide[m][:, :kv_width] for m in range(micro_count)]
    value_wide = [kv_wide[m][:, kv_width:] for m in range(micro_count)]

    doc_ends = jnp.cumsum(lengths, axis=1)
    doc_starts = doc_ends - lengths
    seeds = []
    for m in range(micro_count):
        onehot = (
            (own_pos[:, None] >= doc_starts[m][None, :]) & (own_pos[:, None] < doc_ends[m][None, :])
        ).astype(jnp.float32)
        picked = jnp.dot(onehot, cotangent[m], precision=lax.Precision.HIGHEST)
        doc_length = jnp.dot(
            onehot, lengths[m].astype(jnp.float32), precision=lax.Precision.HIGHEST
        )
        seeds.append((picked / doc_length[:, None]).astype(jnp.bfloat16))

    received = jnp.zeros((tok_rows, feat_width), jnp.bfloat16)
    grad_stream = jnp.zeros((slots, tok_rows, feat_width), jnp.bfloat16)
    kv_total = jnp.zeros((slots, tok_rows, 2 * kv_width), jnp.float32)
    kv_sent = jnp.zeros((slots, wide_rows - tok_rows, 2 * kv_width), jnp.bfloat16)
    gain_total = jnp.zeros((feat_width,), jnp.float32)
    returned_kv = [jnp.zeros((tok_rows, 2 * kv_width), jnp.float32) for _ in range(micro_count)]
    for time_step in range(time_steps):
        raw_index = time_step - (last_segment - section)
        working_buffer = (raw_index >= 0) & (raw_index < micro_count)
        microbatch_index = jnp.clip(raw_index, 0, micro_count - 1)
        slot = jnp.where(working_buffer, microbatch_index, micro_count)
        out_grad = jnp.where(
            section == last_segment, pick(seeds, microbatch_index), received
        )
        stream_grad, gain_part, key_grad, value_grad = attn_bwd(
            lax.dynamic_index_in_dim(stream_store, microbatch_index, 0, keepdims=False),
            gain_row[None],
            out_grad,
            lax.dynamic_index_in_dim(attended_store, microbatch_index, 0, keepdims=False),
            pick(key_wide, microbatch_index),
            pick(value_wide, microbatch_index),
            lax.dynamic_index_in_dim(log_store, microbatch_index, 0, keepdims=False),
            pick(lower_all, microbatch_index),
            upper,
            key_row,
        )
        kv_grad = jnp.concatenate([key_grad, value_grad], axis=-1)
        gain_total = gain_total + jnp.where(working_buffer, gain_part, 0.0)
        grad_stream = lax.dynamic_update_index_in_dim(grad_stream, stream_grad, slot, 0)
        if time_step < time_steps - 1:
            received = shifted(stream_grad, "pipe", -1)
        kv_total = lax.dynamic_update_index_in_dim(
            kv_total, kv_grad[SPAN * tok_rows :], slot, 0
        )
        kv_sent = lax.dynamic_update_index_in_dim(
            kv_sent, kv_grad[: SPAN * tok_rows].astype(jnp.bfloat16), slot, 0
        )
        for m in range(micro_count):
            if time_step == m + segment_count - 1:
                for distance in range(1, SPAN + 1):
                    lo = (SPAN - distance) * tok_rows
                    returned = shifted(kv_sent[m, lo : lo + tok_rows], "ctx", -distance)
                    returned_kv[m] = returned_kv[m] + returned.astype(jnp.float32)

    kv_out = (kv_total[:micro_count] + jnp.stack(returned_kv)).astype(jnp.bfloat16)
    gain_sum = butterfly_sum(gain_total, "ctx")
    return (
        grad_stream[:micro_count][None],
        kv_out[:, :, :kv_width][None],
        kv_out[:, :, kv_width:][None],
        gain_sum.reshape(1, feat_width),
    )


def solution(mesh):
    placed = (
        P(None, "ctx", None),
        P("pipe", None),
        P("pipe", None, "ctx", None),
        P("pipe", None, "ctx", None),
        P(),
        P(),
        P(None, "ctx"),
        P(),
    )
    return jax.shard_map(
        per_device,
        mesh=mesh,
        in_specs=placed,
        out_specs=(
            P("pipe", None, "ctx", None),
            P("pipe", None, "ctx", None),
            P("pipe", None, "ctx", None),
            P("pipe", None),
        ),
        check_vma=False,
    )
```

```python
import functools

import jax
import jax.numpy as jnp
from jax import lax
from jax.experimental import pallas as pl
from jax.experimental.pallas import tpu as pltpu
from jax.sharding import PartitionSpec as P

HEAD_DIM = 128
SPAN = 2
CHUNKS = 1


NORM_EPS = 1e-05


def shifted(x, axis, by):
    size = lax.axis_size(axis)
    pairs = [(i, i + by) for i in range(size) if 0 <= i + by < size]
    return lax.ppermute(x, axis, pairs)


def butterfly_sum(x, axis):
    size = lax.axis_size(axis)
    radices = []
    rest = size
    while rest % 4 == 0:
        radices.append(4)
        rest //= 4
    while rest % 2 == 0:
        radices.append(2)
        rest //= 2
    if rest != 1:
        return lax.psum(x, axis)
    me = lax.axis_index(axis)
    stride = 1
    for radix in radices:
        digit = (me // stride) % radix
        got = [x]
        for offset in range(1, radix):
            pairs = []
            for i in range(size):
                d = (i // stride) % radix
                pairs.append((i, i + (((d - offset) % radix) - d) * stride))
            got.append(lax.ppermute(x, axis, pairs))
        placed = []
        for a in range(radix):
            pick_a = got[0]
            for offset in range(1, radix):
                pick_a = jnp.where((a - digit) % radix == offset, got[offset], pick_a)
            placed.append(pick_a)
        while len(placed) > 1:
            placed = [placed[i] + placed[i + 1] for i in range(0, len(placed), 2)]
        x = placed[0]
        stride *= radix
    return x


NT = (((1,), (1,)), ((), ()))
TN = (((0,), (0,)), ((), ()))

def norm_in_kernel(stream_ref, gain_ref):
    values_f = stream_ref[...].astype(jnp.float32)
    inv_rms = lax.rsqrt(jnp.mean(values_f * values_f, axis=1, keepdims=True) + NORM_EPS)
    normed = values_f * inv_rms
    return values_f, inv_rms, normed, (normed * gain_ref[...]).astype(jnp.bfloat16)


def fwd_kernel(x_ref, gain_ref, k_ref, v_ref, lo_ref, hi_ref, kp_ref, out_ref, o_ref, lt_ref, *, heads, share, scale):
    values_f, _, _, queries = norm_in_kernel(x_ref, gain_ref)
    rows = x_ref.shape[0]
    kpos = kp_ref[...]
    allowed = ((kpos >= lo_ref[...]) & (kpos <= hi_ref[...]))[None]
    for g in range(heads // share):
        gs = slice(g * HEAD_DIM, (g + 1) * HEAD_DIM)
        members = range(g * share, (g + 1) * share)
        q = jnp.concatenate([queries[:, h * HEAD_DIM : (h + 1) * HEAD_DIM] for h in members], axis=0)
        s = lax.dot_general(q, k_ref[:, gs], NT, preferred_element_type=jnp.float32) * scale
        s = s.reshape(share, rows, s.shape[-1])
        tot = jnp.sum(jnp.where(allowed, jnp.exp(s), 0.0), axis=2, keepdims=True)
        lt = jnp.log(tot)
        w = jnp.where(allowed, jnp.exp(s - lt), 0.0).astype(jnp.bfloat16)
        o = jnp.dot(w.reshape(share * rows, -1), v_ref[:, gs], preferred_element_type=jnp.float32)
        for j, h in enumerate(members):
            hs = slice(h * HEAD_DIM, (h + 1) * HEAD_DIM)
            att = o[j * rows : (j + 1) * rows].astype(jnp.bfloat16)
            o_ref[:, hs] = att
            out_ref[:, hs] = (values_f[:, hs] + att.astype(jnp.float32)).astype(out_ref.dtype)
            lt_ref[:, h : h + 1] = lt[j]


def bwd_kernel(x_ref, gain_ref, do_ref, att_ref, k_ref, v_ref, lt_ref, lo_ref, hi_ref, kp_ref, sg_ref, gp_ref, dk_ref, dv_ref, dq_ref, *, heads, share, scale):
    _, inv_rms, normed, queries = norm_in_kernel(x_ref, gain_ref)
    rows = x_ref.shape[0]
    kpos = kp_ref[...]
    allowed = ((kpos >= lo_ref[...]) & (kpos <= hi_ref[...]))[None]
    for g in range(heads // share):
        gs = slice(g * HEAD_DIM, (g + 1) * HEAD_DIM)
        members = range(g * share, (g + 1) * share)
        cols = [slice(h * HEAD_DIM, (h + 1) * HEAD_DIM) for h in members]
        q = jnp.concatenate([queries[:, c] for c in cols], axis=0)
        do = jnp.concatenate([do_ref[:, c] for c in cols], axis=0)
        att = jnp.concatenate([att_ref[:, c] for c in cols], axis=0)
        lt = jnp.stack([lt_ref[:, h : h + 1] for h in members])
        k = k_ref[:, gs]
        v = v_ref[:, gs]
        od = jnp.sum(do.astype(jnp.float32) * att.astype(jnp.float32), axis=1, keepdims=True)
        s = lax.dot_general(q, k, NT, preferred_element_type=jnp.float32) * scale
        s = s.reshape(share, rows, s.shape[-1])
        p = jnp.where(allowed, jnp.exp(s - lt), 0.0).reshape(share * rows, -1)
        dp = lax.dot_general(do, v, NT, preferred_element_type=jnp.float32)
        ds = (p * (dp - od) * scale).astype(jnp.bfloat16)
        w = p.astype(jnp.bfloat16)
        dq = jnp.dot(ds, k, preferred_element_type=jnp.float32)
        for j, c in enumerate(cols):
            dq_ref[:, c] = dq[j * rows : (j + 1) * rows]
        dk_ref[:, gs] = lax.dot_general(ds, q, TN, preferred_element_type=jnp.float32)
        dv_ref[:, gs] = lax.dot_general(w, do, TN, preferred_element_type=jnp.float32)
    query_grad = dq_ref[...]
    gp_ref[...] = jnp.sum(query_grad * normed, axis=0, keepdims=True)
    normed_grad = query_grad * gain_ref[...]
    norm_grad = inv_rms * (
        normed_grad - normed * jnp.mean(normed_grad * normed, axis=1, keepdims=True)
    )
    sg_ref[...] = (do_ref[...].astype(jnp.float32) + norm_grad).astype(sg_ref.dtype)


def attn_fwd(x, gain, k, v, lo, hi, kp):
    rows, width = x.shape
    heads = width // HEAD_DIM
    share = heads // (k.shape[1] // HEAD_DIM)
    kern = functools.partial(fwd_kernel, heads=heads, share=share, scale=HEAD_DIM ** -0.5)
    return pl.pallas_call(
        kern,
        out_shape=(
            jax.ShapeDtypeStruct((rows, width), jnp.bfloat16),
            jax.ShapeDtypeStruct((rows, width), jnp.bfloat16),
            jax.ShapeDtypeStruct((rows, heads), jnp.float32),
        ),
    )(x, gain, k, v, lo, hi, kp)


def attn_bwd(x, gain, do, att, k, v, lt, lo, hi, kp):
    rows, width = x.shape
    heads = width // HEAD_DIM
    share = heads // (k.shape[1] // HEAD_DIM)
    kern = functools.partial(bwd_kernel, heads=heads, share=share, scale=HEAD_DIM ** -0.5)
    sg, gp, dk, dv = pl.pallas_call(
        kern,
        out_shape=(
            jax.ShapeDtypeStruct((rows, width), jnp.bfloat16),
            jax.ShapeDtypeStruct((1, width), jnp.float32),
            jax.ShapeDtypeStruct(k.shape, jnp.float32),
            jax.ShapeDtypeStruct(v.shape, jnp.float32),
        ),
        scratch_shapes=[pltpu.VMEM((rows, width), jnp.float32)],
    )(x, gain, do, att, k, v, lt, lo, hi, kp)
    return sg, gp[0], dk, dv


def per_device(hidden, gain, keys, values, cotangent, lengths, doc_start, block_mask):
    section = lax.axis_index("pipe")
    segment_count = lax.axis_size("pipe")
    index_of_block = lax.axis_index("ctx")
    micro_count, tok_rows, feat_width = hidden.shape
    kv_width = keys.shape[3]
    groups = kv_width // HEAD_DIM
    group_share = feat_width // HEAD_DIM // groups
    gain_row = gain[0]
    last_segment = segment_count - 1
    offsets = jnp.arange(tok_rows, dtype=jnp.int32)
    own_pos = index_of_block * tok_rows + offsets
    wide_rows = (SPAN + 1) * tok_rows
    key_pos = (index_of_block - SPAN) * tok_rows + jnp.arange(wide_rows, dtype=jnp.int32)
    time_steps = micro_count + segment_count - 1

    kv_own = jnp.concatenate([keys[0], values[0]], axis=-1)
    def window_of(own):
        return jnp.concatenate(
            [shifted(own, "ctx", distance) for distance in range(SPAN, 0, -1)] + [own]
        )

    kv_wide = [window_of(kv_own[0])] + [None] * (micro_count - 1)
    lower_all = [doc_start[m][:, None] for m in range(micro_count)]
    upper = own_pos[:, None]
    key_row = key_pos[None, :]

    def pick(items, index):
        out = items[0]
        for m in range(1, len(items)):
            out = jnp.where(index == m, items[m], out)
        return out

    slots = micro_count + 1
    received = jnp.zeros((tok_rows, feat_width), jnp.bfloat16)
    stream_store = jnp.zeros((slots, tok_rows, feat_width), jnp.bfloat16)
    attended_store = jnp.zeros((slots, tok_rows, feat_width), jnp.bfloat16)
    log_store = jnp.zeros((slots, tok_rows, groups * group_share), jnp.float32)
    for time_step in range(time_steps):
        raw_index = time_step - section
        working_buffer = (raw_index >= 0) & (raw_index < micro_count)
        microbatch_index = jnp.clip(raw_index, 0, micro_count - 1)
        slot = jnp.where(working_buffer, microbatch_index, micro_count)
        ready = [m for m in range(micro_count) if kv_wide[m] is not None]
        window = pick([kv_wide[m] for m in ready], jnp.minimum(microbatch_index, len(ready) - 1))
        stream_in = jnp.where(section == 0, hidden[microbatch_index], received)
        stream_out, attended, log_total = attn_fwd(
            stream_in,
            gain_row[None],
            window[:, :kv_width],
            window[:, kv_width:],
            pick(lower_all, microbatch_index),
            upper,
            key_row,
        )
        for m in range(micro_count):
            if kv_wide[m] is None and m == time_step + 1:
                tied, _ = lax.optimization_barrier((kv_own[m], attended))
                kv_wide[m] = window_of(tied)
        stream_store = lax.dynamic_update_index_in_dim(stream_store, stream_in, slot, 0)
        attended_store = lax.dynamic_update_index_in_dim(attended_store, attended, slot, 0)
        log_store = lax.dynamic_update_index_in_dim(log_store, log_total, slot, 0)
        if time_step < time_steps - 1:
            received = shifted(stream_out, "pipe", 1)
    key_wide = [kv_wide[m][:, :kv_width] for m in range(micro_count)]
    value_wide = [kv_wide[m][:, kv_width:] for m in range(micro_count)]

    doc_ends = jnp.cumsum(lengths, axis=1)
    doc_starts = doc_ends - lengths
    seeds = []
    for m in range(micro_count):
        onehot = (
            (own_pos[:, None] >= doc_starts[m][None, :]) & (own_pos[:, None] < doc_ends[m][None, :])
        ).astype(jnp.float32)
        picked = jnp.dot(onehot, cotangent[m], precision=lax.Precision.HIGHEST)
        doc_length = jnp.dot(
            onehot, lengths[m].astype(jnp.float32), precision=lax.Precision.HIGHEST
        )
        seeds.append((picked / doc_length[:, None]).astype(jnp.bfloat16))

    received = jnp.zeros((tok_rows, feat_width), jnp.bfloat16)
    grad_stream = jnp.zeros((slots, tok_rows, feat_width), jnp.bfloat16)
    kv_total = jnp.zeros((slots, tok_rows, 2 * kv_width), jnp.float32)
    kv_sent = jnp.zeros((slots, wide_rows - tok_rows, 2 * kv_width), jnp.bfloat16)
    gain_total = jnp.zeros((feat_width,), jnp.float32)
    returned_kv = [jnp.zeros((tok_rows, 2 * kv_width), jnp.float32) for _ in range(micro_count)]
    for time_step in range(time_steps):
        raw_index = time_step - (last_segment - section)
        working_buffer = (raw_index >= 0) & (raw_index < micro_count)
        microbatch_index = jnp.clip(raw_index, 0, micro_count - 1)
        slot = jnp.where(working_buffer, microbatch_index, micro_count)
        out_grad = jnp.where(
            section == last_segment, pick(seeds, microbatch_index), received
        )
        stream_grad, gain_part, key_grad, value_grad = attn_bwd(
            lax.dynamic_index_in_dim(stream_store, microbatch_index, 0, keepdims=False),
            gain_row[None],
            out_grad,
            lax.dynamic_index_in_dim(attended_store, microbatch_index, 0, keepdims=False),
            pick(key_wide, microbatch_index),
            pick(value_wide, microbatch_index),
            lax.dynamic_index_in_dim(log_store, microbatch_index, 0, keepdims=False),
            pick(lower_all, microbatch_index),
            upper,
            key_row,
        )
        kv_grad = jnp.concatenate([key_grad, value_grad], axis=-1)
        gain_total = gain_total + jnp.where(working_buffer, gain_part, 0.0)
        grad_stream = lax.dynamic_update_index_in_dim(grad_stream, stream_grad, slot, 0)
        if time_step < time_steps - 1:
            received = shifted(stream_grad, "pipe", -1)
        kv_total = lax.dynamic_update_index_in_dim(
            kv_total, kv_grad[SPAN * tok_rows :], slot, 0
        )
        kv_sent = lax.dynamic_update_index_in_dim(
            kv_sent, kv_grad[: SPAN * tok_rows].astype(jnp.bfloat16), slot, 0
        )
        for m in range(micro_count):
            if time_step == m + segment_count - 1:
                for distance in range(1, SPAN + 1):
                    lo = (SPAN - distance) * tok_rows
                    returned = shifted(kv_sent[m, lo : lo + tok_rows], "ctx", -distance)
                    returned_kv[m] = returned_kv[m] + returned.astype(jnp.float32)

    kv_out = (kv_total[:micro_count] + jnp.stack(returned_kv)).astype(jnp.bfloat16)
    gain_sum = jnp.sum(lax.all_gather(gain_total, "ctx"), axis=0)
    return (
        grad_stream[:micro_count][None],
        kv_out[:, :, :kv_width][None],
        kv_out[:, :, kv_width:][None],
        gain_sum.reshape(1, feat_width),
    )


def solution(mesh):
    placed = (
        P(None, "ctx", None),
        P("pipe", None),
        P("pipe", None, "ctx", None),
        P("pipe", None, "ctx", None),
        P(),
        P(),
        P(None, "ctx"),
        P(),
    )
    return jax.shard_map(
        per_device,
        mesh=mesh,
        in_specs=placed,
        out_specs=(
            P("pipe", None, "ctx", None),
            P("pipe", None, "ctx", None),
            P("pipe", None, "ctx", None),
            P("pipe", None),
        ),
        check_vma=False,
    )
```

```python
import functools

import jax
import jax.numpy as jnp
from jax import lax
from jax.experimental import pallas as pl
from jax.experimental.pallas import tpu as pltpu
from jax.sharding import PartitionSpec as P

HEAD_DIM = 128
SPAN = 2
CHUNKS = 1


NORM_EPS = 1e-05


def shifted(x, axis, by):
    size = lax.axis_size(axis)
    pairs = [(i, i + by) for i in range(size) if 0 <= i + by < size]
    return lax.ppermute(x, axis, pairs)


def butterfly_sum(x, axis):
    size = lax.axis_size(axis)
    radices = []
    rest = size
    while rest % 8 == 0:
        radices.append(8)
        rest //= 8
    while rest % 4 == 0:
        radices.append(4)
        rest //= 4
    while rest % 2 == 0:
        radices.append(2)
        rest //= 2
    if rest != 1:
        return lax.psum(x, axis)
    me = lax.axis_index(axis)
    stride = 1
    for radix in radices:
        digit = (me // stride) % radix
        got = [x]
        for offset in range(1, radix):
            pairs = []
            for i in range(size):
                d = (i // stride) % radix
                pairs.append((i, i + (((d - offset) % radix) - d) * stride))
            got.append(lax.ppermute(x, axis, pairs))
        placed = []
        for a in range(radix):
            pick_a = got[0]
            for offset in range(1, radix):
                pick_a = jnp.where((a - digit) % radix == offset, got[offset], pick_a)
            placed.append(pick_a)
        while len(placed) > 1:
            placed = [placed[i] + placed[i + 1] for i in range(0, len(placed), 2)]
        x = placed[0]
        stride *= radix
    return x


NT = (((1,), (1,)), ((), ()))
TN = (((0,), (0,)), ((), ()))

def norm_in_kernel(stream_ref, gain_ref):
    values_f = stream_ref[...].astype(jnp.float32)
    inv_rms = lax.rsqrt(jnp.mean(values_f * values_f, axis=1, keepdims=True) + NORM_EPS)
    normed = values_f * inv_rms
    return values_f, inv_rms, normed, (normed * gain_ref[...]).astype(jnp.bfloat16)


def fwd_kernel(x_ref, gain_ref, k_ref, v_ref, lo_ref, hi_ref, kp_ref, out_ref, o_ref, lt_ref, *, heads, share, scale):
    values_f, _, _, queries = norm_in_kernel(x_ref, gain_ref)
    rows = x_ref.shape[0]
    kpos = kp_ref[...]
    allowed = ((kpos >= lo_ref[...]) & (kpos <= hi_ref[...]))[None]
    for g in range(heads // share):
        gs = slice(g * HEAD_DIM, (g + 1) * HEAD_DIM)
        members = range(g * share, (g + 1) * share)
        q = jnp.concatenate([queries[:, h * HEAD_DIM : (h + 1) * HEAD_DIM] for h in members], axis=0)
        s = lax.dot_general(q, k_ref[:, gs], NT, preferred_element_type=jnp.float32) * scale
        s = s.reshape(share, rows, s.shape[-1])
        tot = jnp.sum(jnp.where(allowed, jnp.exp(s), 0.0), axis=2, keepdims=True)
        lt = jnp.log(tot)
        w = jnp.where(allowed, jnp.exp(s - lt), 0.0).astype(jnp.bfloat16)
        o = jnp.dot(w.reshape(share * rows, -1), v_ref[:, gs], preferred_element_type=jnp.float32)
        for j, h in enumerate(members):
            hs = slice(h * HEAD_DIM, (h + 1) * HEAD_DIM)
            att = o[j * rows : (j + 1) * rows].astype(jnp.bfloat16)
            o_ref[:, hs] = att
            out_ref[:, hs] = (values_f[:, hs] + att.astype(jnp.float32)).astype(out_ref.dtype)
            lt_ref[:, h : h + 1] = lt[j]


def bwd_kernel(x_ref, gain_ref, do_ref, att_ref, k_ref, v_ref, lt_ref, lo_ref, hi_ref, kp_ref, sg_ref, gp_ref, dk_ref, dv_ref, dq_ref, *, heads, share, scale):
    _, inv_rms, normed, queries = norm_in_kernel(x_ref, gain_ref)
    rows = x_ref.shape[0]
    kpos = kp_ref[...]
    allowed = ((kpos >= lo_ref[...]) & (kpos <= hi_ref[...]))[None]
    for g in range(heads // share):
        gs = slice(g * HEAD_DIM, (g + 1) * HEAD_DIM)
        members = range(g * share, (g + 1) * share)
        cols = [slice(h * HEAD_DIM, (h + 1) * HEAD_DIM) for h in members]
        q = jnp.concatenate([queries[:, c] for c in cols], axis=0)
        do = jnp.concatenate([do_ref[:, c] for c in cols], axis=0)
        att = jnp.concatenate([att_ref[:, c] for c in cols], axis=0)
        lt = jnp.stack([lt_ref[:, h : h + 1] for h in members])
        k = k_ref[:, gs]
        v = v_ref[:, gs]
        od = jnp.sum(do.astype(jnp.float32) * att.astype(jnp.float32), axis=1, keepdims=True)
        s = lax.dot_general(q, k, NT, preferred_element_type=jnp.float32) * scale
        s = s.reshape(share, rows, s.shape[-1])
        p = jnp.where(allowed, jnp.exp(s - lt), 0.0).reshape(share * rows, -1)
        dp = lax.dot_general(do, v, NT, preferred_element_type=jnp.float32)
        ds = (p * (dp - od) * scale).astype(jnp.bfloat16)
        w = p.astype(jnp.bfloat16)
        dq = jnp.dot(ds, k, preferred_element_type=jnp.float32)
        for j, c in enumerate(cols):
            dq_ref[:, c] = dq[j * rows : (j + 1) * rows]
        dk_ref[:, gs] = lax.dot_general(ds, q, TN, preferred_element_type=jnp.float32)
        dv_ref[:, gs] = lax.dot_general(w, do, TN, preferred_element_type=jnp.float32)
    query_grad = dq_ref[...]
    gp_ref[...] = jnp.sum(query_grad * normed, axis=0, keepdims=True)
    normed_grad = query_grad * gain_ref[...]
    norm_grad = inv_rms * (
        normed_grad - normed * jnp.mean(normed_grad * normed, axis=1, keepdims=True)
    )
    sg_ref[...] = (do_ref[...].astype(jnp.float32) + norm_grad).astype(sg_ref.dtype)


def attn_fwd(x, gain, k, v, lo, hi, kp):
    rows, width = x.shape
    heads = width // HEAD_DIM
    share = heads // (k.shape[1] // HEAD_DIM)
    kern = functools.partial(fwd_kernel, heads=heads, share=share, scale=HEAD_DIM ** -0.5)
    return pl.pallas_call(
        kern,
        out_shape=(
            jax.ShapeDtypeStruct((rows, width), jnp.bfloat16),
            jax.ShapeDtypeStruct((rows, width), jnp.bfloat16),
            jax.ShapeDtypeStruct((rows, heads), jnp.float32),
        ),
    )(x, gain, k, v, lo, hi, kp)


def attn_bwd(x, gain, do, att, k, v, lt, lo, hi, kp):
    rows, width = x.shape
    heads = width // HEAD_DIM
    share = heads // (k.shape[1] // HEAD_DIM)
    kern = functools.partial(bwd_kernel, heads=heads, share=share, scale=HEAD_DIM ** -0.5)
    sg, gp, dk, dv = pl.pallas_call(
        kern,
        out_shape=(
            jax.ShapeDtypeStruct((rows, width), jnp.bfloat16),
            jax.ShapeDtypeStruct((1, width), jnp.float32),
            jax.ShapeDtypeStruct(k.shape, jnp.float32),
            jax.ShapeDtypeStruct(v.shape, jnp.float32),
        ),
        scratch_shapes=[pltpu.VMEM((rows, width), jnp.float32)],
    )(x, gain, do, att, k, v, lt, lo, hi, kp)
    return sg, gp[0], dk, dv


def per_device(hidden, gain, keys, values, cotangent, lengths, doc_start, block_mask):
    section = lax.axis_index("pipe")
    segment_count = lax.axis_size("pipe")
    index_of_block = lax.axis_index("ctx")
    micro_count, tok_rows, feat_width = hidden.shape
    kv_width = keys.shape[3]
    groups = kv_width // HEAD_DIM
    group_share = feat_width // HEAD_DIM // groups
    gain_row = gain[0]
    last_segment = segment_count - 1
    offsets = jnp.arange(tok_rows, dtype=jnp.int32)
    own_pos = index_of_block * tok_rows + offsets
    wide_rows = (SPAN + 1) * tok_rows
    key_pos = (index_of_block - SPAN) * tok_rows + jnp.arange(wide_rows, dtype=jnp.int32)
    time_steps = micro_count + segment_count - 1

    kv_own = jnp.concatenate([keys[0], values[0]], axis=-1)
    def window_of(own):
        return jnp.concatenate(
            [shifted(own, "ctx", distance) for distance in range(SPAN, 0, -1)] + [own]
        )

    kv_wide = [window_of(kv_own[0])] + [None] * (micro_count - 1)
    lower_all = [doc_start[m][:, None] for m in range(micro_count)]
    upper = own_pos[:, None]
    key_row = key_pos[None, :]

    def pick(items, index):
        out = items[0]
        for m in range(1, len(items)):
            out = jnp.where(index == m, items[m], out)
        return out

    slots = micro_count + 1
    received = jnp.zeros((tok_rows, feat_width), jnp.bfloat16)
    stream_store = jnp.zeros((slots, tok_rows, feat_width), jnp.bfloat16)
    attended_store = jnp.zeros((slots, tok_rows, feat_width), jnp.bfloat16)
    log_store = jnp.zeros((slots, tok_rows, groups * group_share), jnp.float32)
    for time_step in range(time_steps):
        raw_index = time_step - section
        working_buffer = (raw_index >= 0) & (raw_index < micro_count)
        microbatch_index = jnp.clip(raw_index, 0, micro_count - 1)
        slot = jnp.where(working_buffer, microbatch_index, micro_count)
        ready = [m for m in range(micro_count) if kv_wide[m] is not None]
        window = pick([kv_wide[m] for m in ready], jnp.minimum(microbatch_index, len(ready) - 1))
        stream_in = jnp.where(section == 0, hidden[microbatch_index], received)
        stream_out, attended, log_total = attn_fwd(
            stream_in,
            gain_row[None],
            window[:, :kv_width],
            window[:, kv_width:],
            pick(lower_all, microbatch_index),
            upper,
            key_row,
        )
        for m in range(micro_count):
            if kv_wide[m] is None and m == time_step + 1:
                tied, _ = lax.optimization_barrier((kv_own[m], attended))
                kv_wide[m] = window_of(tied)
        stream_store = lax.dynamic_update_index_in_dim(stream_store, stream_in, slot, 0)
        attended_store = lax.dynamic_update_index_in_dim(attended_store, attended, slot, 0)
        log_store = lax.dynamic_update_index_in_dim(log_store, log_total, slot, 0)
        if time_step < time_steps - 1:
            received = shifted(stream_out, "pipe", 1)
    key_wide = [kv_wide[m][:, :kv_width] for m in range(micro_count)]
    value_wide = [kv_wide[m][:, kv_width:] for m in range(micro_count)]

    doc_ends = jnp.cumsum(lengths, axis=1)
    doc_starts = doc_ends - lengths
    seeds = []
    for m in range(micro_count):
        onehot = (
            (own_pos[:, None] >= doc_starts[m][None, :]) & (own_pos[:, None] < doc_ends[m][None, :])
        ).astype(jnp.float32)
        picked = jnp.dot(onehot, cotangent[m], precision=lax.Precision.HIGHEST)
        doc_length = jnp.dot(
            onehot, lengths[m].astype(jnp.float32), precision=lax.Precision.HIGHEST
        )
        seeds.append((picked / doc_length[:, None]).astype(jnp.bfloat16))

    received = jnp.zeros((tok_rows, feat_width), jnp.bfloat16)
    grad_stream = jnp.zeros((slots, tok_rows, feat_width), jnp.bfloat16)
    kv_total = jnp.zeros((slots, tok_rows, 2 * kv_width), jnp.float32)
    kv_sent = jnp.zeros((slots, wide_rows - tok_rows, 2 * kv_width), jnp.bfloat16)
    gain_total = jnp.zeros((feat_width,), jnp.float32)
    returned_kv = [jnp.zeros((tok_rows, 2 * kv_width), jnp.float32) for _ in range(micro_count)]
    for time_step in range(time_steps):
        raw_index = time_step - (last_segment - section)
        working_buffer = (raw_index >= 0) & (raw_index < micro_count)
        microbatch_index = jnp.clip(raw_index, 0, micro_count - 1)
        slot = jnp.where(working_buffer, microbatch_index, micro_count)
        out_grad = jnp.where(
            section == last_segment, pick(seeds, microbatch_index), received
        )
        stream_grad, gain_part, key_grad, value_grad = attn_bwd(
            lax.dynamic_index_in_dim(stream_store, microbatch_index, 0, keepdims=False),
            gain_row[None],
            out_grad,
            lax.dynamic_index_in_dim(attended_store, microbatch_index, 0, keepdims=False),
            pick(key_wide, microbatch_index),
            pick(value_wide, microbatch_index),
            lax.dynamic_index_in_dim(log_store, microbatch_index, 0, keepdims=False),
            pick(lower_all, microbatch_index),
            upper,
            key_row,
        )
        kv_grad = jnp.concatenate([key_grad, value_grad], axis=-1)
        gain_total = gain_total + jnp.where(working_buffer, gain_part, 0.0)
        grad_stream = lax.dynamic_update_index_in_dim(grad_stream, stream_grad, slot, 0)
        if time_step < time_steps - 1:
            received = shifted(stream_grad, "pipe", -1)
        kv_total = lax.dynamic_update_index_in_dim(
            kv_total, kv_grad[SPAN * tok_rows :], slot, 0
        )
        kv_sent = lax.dynamic_update_index_in_dim(
            kv_sent, kv_grad[: SPAN * tok_rows].astype(jnp.bfloat16), slot, 0
        )
        for m in range(micro_count):
            if time_step == m + segment_count - 1:
                for distance in range(1, SPAN + 1):
                    lo = (SPAN - distance) * tok_rows
                    returned = shifted(kv_sent[m, lo : lo + tok_rows], "ctx", -distance)
                    returned_kv[m] = returned_kv[m] + returned.astype(jnp.float32)

    kv_out = (kv_total[:micro_count] + jnp.stack(returned_kv)).astype(jnp.bfloat16)
    gain_sum = butterfly_sum(gain_total, "ctx")
    return (
        grad_stream[:micro_count][None],
        kv_out[:, :, :kv_width][None],
        kv_out[:, :, kv_width:][None],
        gain_sum.reshape(1, feat_width),
    )


def solution(mesh):
    placed = (
        P(None, "ctx", None),
        P("pipe", None),
        P("pipe", None, "ctx", None),
        P("pipe", None, "ctx", None),
        P(),
        P(),
        P(None, "ctx"),
        P(),
    )
    return jax.shard_map(
        per_device,
        mesh=mesh,
        in_specs=placed,
        out_specs=(
            P("pipe", None, "ctx", None),
            P("pipe", None, "ctx", None),
            P("pipe", None, "ctx", None),
            P("pipe", None),
        ),
        check_vma=False,
    )
```

```python
import functools

import jax
import jax.numpy as jnp
from jax import lax
from jax.experimental import pallas as pl
from jax.experimental.pallas import tpu as pltpu
from jax.sharding import PartitionSpec as P

HEAD_DIM = 128
SPAN = 2
CHUNKS = 1


NORM_EPS = 1e-05


def shifted(x, axis, by):
    size = lax.axis_size(axis)
    pairs = [(i, i + by) for i in range(size) if 0 <= i + by < size]
    return lax.ppermute(x, axis, pairs)


def butterfly_sum(x, axis):
    size = lax.axis_size(axis)
    radices = []
    rest = size
    while rest % 4 == 0:
        radices.append(4)
        rest //= 4
    while rest % 2 == 0:
        radices.append(2)
        rest //= 2
    if rest != 1:
        return lax.psum(x, axis)
    me = lax.axis_index(axis)
    stride = 1
    for radix in radices:
        digit = (me // stride) % radix
        got = [x]
        for offset in range(1, radix):
            pairs = []
            for i in range(size):
                d = (i // stride) % radix
                pairs.append((i, i + (((d - offset) % radix) - d) * stride))
            got.append(lax.ppermute(x, axis, pairs))
        placed = []
        for a in range(radix):
            pick_a = got[0]
            for offset in range(1, radix):
                pick_a = jnp.where((a - digit) % radix == offset, got[offset], pick_a)
            placed.append(pick_a)
        while len(placed) > 1:
            placed = [placed[i] + placed[i + 1] for i in range(0, len(placed), 2)]
        x = placed[0]
        stride *= radix
    return x


NT = (((1,), (1,)), ((), ()))
TN = (((0,), (0,)), ((), ()))

def norm_in_kernel(stream_ref, gain_ref):
    values_f = stream_ref[...].astype(jnp.float32)
    inv_rms = lax.rsqrt(jnp.mean(values_f * values_f, axis=1, keepdims=True) + NORM_EPS)
    normed = values_f * inv_rms
    return values_f, inv_rms, normed, (normed * gain_ref[...]).astype(jnp.bfloat16)


def fwd_kernel(x_ref, gain_ref, k_ref, v_ref, lo_ref, hi_ref, kp_ref, out_ref, o_ref, lt_ref, *, heads, share, scale):
    values_f, _, _, queries = norm_in_kernel(x_ref, gain_ref)
    rows = x_ref.shape[0]
    kpos = kp_ref[...]
    allowed = ((kpos >= lo_ref[...]) & (kpos <= hi_ref[...]))[None]
    for g in range(heads // share):
        gs = slice(g * HEAD_DIM, (g + 1) * HEAD_DIM)
        members = range(g * share, (g + 1) * share)
        q = jnp.concatenate([queries[:, h * HEAD_DIM : (h + 1) * HEAD_DIM] for h in members], axis=0)
        s = lax.dot_general(q, k_ref[:, gs], NT, preferred_element_type=jnp.float32) * scale
        s = s.reshape(share, rows, s.shape[-1])
        tot = jnp.sum(jnp.where(allowed, jnp.exp(s), 0.0), axis=2, keepdims=True)
        lt = jnp.log(tot)
        w = jnp.where(allowed, jnp.exp(s - lt), 0.0).astype(jnp.bfloat16)
        o = jnp.dot(w.reshape(share * rows, -1), v_ref[:, gs], preferred_element_type=jnp.float32)
        for j, h in enumerate(members):
            hs = slice(h * HEAD_DIM, (h + 1) * HEAD_DIM)
            att = o[j * rows : (j + 1) * rows].astype(jnp.bfloat16)
            o_ref[:, hs] = att
            out_ref[:, hs] = (values_f[:, hs] + att.astype(jnp.float32)).astype(out_ref.dtype)
            lt_ref[:, h : h + 1] = lt[j]


def bwd_kernel(x_ref, gain_ref, do_ref, att_ref, k_ref, v_ref, lt_ref, lo_ref, hi_ref, kp_ref, sg_ref, gp_ref, dk_ref, dv_ref, dq_ref, *, heads, share, scale):
    _, inv_rms, normed, queries = norm_in_kernel(x_ref, gain_ref)
    rows = x_ref.shape[0]
    kpos = kp_ref[...]
    allowed = ((kpos >= lo_ref[...]) & (kpos <= hi_ref[...]))[None]
    for g in range(heads // share):
        gs = slice(g * HEAD_DIM, (g + 1) * HEAD_DIM)
        members = range(g * share, (g + 1) * share)
        cols = [slice(h * HEAD_DIM, (h + 1) * HEAD_DIM) for h in members]
        q = jnp.concatenate([queries[:, c] for c in cols], axis=0)
        do = jnp.concatenate([do_ref[:, c] for c in cols], axis=0)
        att = jnp.concatenate([att_ref[:, c] for c in cols], axis=0)
        lt = jnp.stack([lt_ref[:, h : h + 1] for h in members])
        k = k_ref[:, gs]
        v = v_ref[:, gs]
        od = jnp.sum(do.astype(jnp.float32) * att.astype(jnp.float32), axis=1, keepdims=True)
        s = lax.dot_general(q, k, NT, preferred_element_type=jnp.float32) * scale
        s = s.reshape(share, rows, s.shape[-1])
        p = jnp.where(allowed, jnp.exp(s - lt), 0.0).reshape(share * rows, -1)
        dp = lax.dot_general(do, v, NT, preferred_element_type=jnp.float32)
        ds = (p * (dp - od) * scale).astype(jnp.bfloat16)
        w = p.astype(jnp.bfloat16)
        dq = jnp.dot(ds, k, preferred_element_type=jnp.float32)
        for j, c in enumerate(cols):
            dq_ref[:, c] = dq[j * rows : (j + 1) * rows]
        dk_ref[:, gs] = lax.dot_general(ds, q, TN, preferred_element_type=jnp.float32)
        dv_ref[:, gs] = lax.dot_general(w, do, TN, preferred_element_type=jnp.float32)
    query_grad = dq_ref[...]
    gp_ref[...] = jnp.sum(query_grad * normed, axis=0, keepdims=True)
    normed_grad = query_grad * gain_ref[...]
    norm_grad = inv_rms * (
        normed_grad - normed * jnp.mean(normed_grad * normed, axis=1, keepdims=True)
    )
    sg_ref[...] = (do_ref[...].astype(jnp.float32) + norm_grad).astype(sg_ref.dtype)


def attn_fwd(x, gain, k, v, lo, hi, kp):
    rows, width = x.shape
    heads = width // HEAD_DIM
    share = heads // (k.shape[1] // HEAD_DIM)
    kern = functools.partial(fwd_kernel, heads=heads, share=share, scale=HEAD_DIM ** -0.5)
    return pl.pallas_call(
        kern,
        out_shape=(
            jax.ShapeDtypeStruct((rows, width), jnp.bfloat16),
            jax.ShapeDtypeStruct((rows, width), jnp.bfloat16),
            jax.ShapeDtypeStruct((rows, heads), jnp.float32),
        ),
    )(x, gain, k, v, lo, hi, kp)


def attn_bwd(x, gain, do, att, k, v, lt, lo, hi, kp):
    rows, width = x.shape
    heads = width // HEAD_DIM
    share = heads // (k.shape[1] // HEAD_DIM)
    kern = functools.partial(bwd_kernel, heads=heads, share=share, scale=HEAD_DIM ** -0.5)
    sg, gp, dk, dv = pl.pallas_call(
        kern,
        out_shape=(
            jax.ShapeDtypeStruct((rows, width), jnp.bfloat16),
            jax.ShapeDtypeStruct((1, width), jnp.float32),
            jax.ShapeDtypeStruct(k.shape, jnp.float32),
            jax.ShapeDtypeStruct(v.shape, jnp.float32),
        ),
        scratch_shapes=[pltpu.VMEM((rows, width), jnp.float32)],
    )(x, gain, do, att, k, v, lt, lo, hi, kp)
    return sg, gp[0], dk, dv


def attn_bwd_at(index, x_all, gain, do, att_all, kv_all, lt_all, lo_all, hi, kp):
    rows, width = do.shape
    heads = width // HEAD_DIM
    wide, kv_both = kv_all.shape[1:]
    half = kv_both // 2
    share = heads // (half // HEAD_DIM)
    kern = functools.partial(bwd_kernel, heads=heads, share=share, scale=HEAD_DIM ** -0.5)

    def whole(shape):
        return pl.BlockSpec(shape, lambda i, s: (0,) * len(shape))

    def slot(shape, last=0):
        return pl.BlockSpec((None,) + shape, lambda i, s: (s[0],) + (0,) * (len(shape) - 1) + (last,))

    grid_spec = pltpu.PrefetchScalarGridSpec(
        num_scalar_prefetch=1,
        grid=(1,),
        in_specs=[
            slot((rows, width)),
            whole(gain.shape),
            whole(do.shape),
            slot((rows, width)),
            slot((wide, half), 0),
            slot((wide, half), 1),
            slot(lt_all.shape[1:]),
            slot(lo_all.shape[1:]),
            whole(hi.shape),
            whole(kp.shape),
        ],
        out_specs=[
            whole((rows, width)),
            whole((1, width)),
            whole((wide, half)),
            whole((wide, half)),
        ],
        scratch_shapes=[pltpu.VMEM((rows, width), jnp.float32)],
    )

    def body(s_ref, *refs):
        kern(*refs)

    sg, gp, dk, dv = pl.pallas_call(
        body,
        grid_spec=grid_spec,
        out_shape=(
            jax.ShapeDtypeStruct((rows, width), jnp.bfloat16),
            jax.ShapeDtypeStruct((1, width), jnp.float32),
            jax.ShapeDtypeStruct((wide, half), jnp.float32),
            jax.ShapeDtypeStruct((wide, half), jnp.float32),
        ),
    )(index, x_all, gain, do, att_all, kv_all, kv_all, lt_all, lo_all, hi, kp)
    return sg, gp[0], dk, dv


def per_device(hidden, gain, keys, values, cotangent, lengths, doc_start, block_mask):
    section = lax.axis_index("pipe")
    segment_count = lax.axis_size("pipe")
    index_of_block = lax.axis_index("ctx")
    micro_count, tok_rows, feat_width = hidden.shape
    kv_width = keys.shape[3]
    groups = kv_width // HEAD_DIM
    group_share = feat_width // HEAD_DIM // groups
    gain_row = gain[0]
    last_segment = segment_count - 1
    offsets = jnp.arange(tok_rows, dtype=jnp.int32)
    own_pos = index_of_block * tok_rows + offsets
    wide_rows = (SPAN + 1) * tok_rows
    key_pos = (index_of_block - SPAN) * tok_rows + jnp.arange(wide_rows, dtype=jnp.int32)
    time_steps = micro_count + segment_count - 1

    kv_own = jnp.concatenate([keys[0], values[0]], axis=-1)
    def window_of(own):
        return jnp.concatenate(
            [shifted(own, "ctx", distance) for distance in range(SPAN, 0, -1)] + [own]
        )

    kv_wide = [window_of(kv_own[0])] + [None] * (micro_count - 1)
    lower_all = [doc_start[m][:, None] for m in range(micro_count)]
    upper = own_pos[:, None]
    key_row = key_pos[None, :]

    def pick(items, index):
        out = items[0]
        for m in range(1, len(items)):
            out = jnp.where(index == m, items[m], out)
        return out

    slots = micro_count + 1
    received = jnp.zeros((tok_rows, feat_width), jnp.bfloat16)
    stream_store = jnp.zeros((slots, tok_rows, feat_width), jnp.bfloat16)
    attended_store = jnp.zeros((slots, tok_rows, feat_width), jnp.bfloat16)
    log_store = jnp.zeros((slots, tok_rows, groups * group_share), jnp.float32)
    for time_step in range(time_steps):
        raw_index = time_step - section
        working_buffer = (raw_index >= 0) & (raw_index < micro_count)
        microbatch_index = jnp.clip(raw_index, 0, micro_count - 1)
        slot = jnp.where(working_buffer, microbatch_index, micro_count)
        ready = [m for m in range(micro_count) if kv_wide[m] is not None]
        window = pick([kv_wide[m] for m in ready], jnp.minimum(microbatch_index, len(ready) - 1))
        stream_in = jnp.where(section == 0, hidden[microbatch_index], received)
        stream_out, attended, log_total = attn_fwd(
            stream_in,
            gain_row[None],
            window[:, :kv_width],
            window[:, kv_width:],
            pick(lower_all, microbatch_index),
            upper,
            key_row,
        )
        for m in range(micro_count):
            if kv_wide[m] is None and m == time_step + 1:
                tied, _ = lax.optimization_barrier((kv_own[m], attended))
                kv_wide[m] = window_of(tied)
        stream_store = lax.dynamic_update_index_in_dim(stream_store, stream_in, slot, 0)
        attended_store = lax.dynamic_update_index_in_dim(attended_store, attended, slot, 0)
        log_store = lax.dynamic_update_index_in_dim(log_store, log_total, slot, 0)
        if time_step < time_steps - 1:
            received = shifted(stream_out, "pipe", 1)
    kv_stack = jnp.stack(kv_wide)
    lower_stack = doc_start[:, :, None]

    doc_ends = jnp.cumsum(lengths, axis=1)
    doc_starts = doc_ends - lengths
    seeds = []
    for m in range(micro_count):
        onehot = (
            (own_pos[:, None] >= doc_starts[m][None, :]) & (own_pos[:, None] < doc_ends[m][None, :])
        ).astype(jnp.float32)
        picked = jnp.dot(onehot, cotangent[m], precision=lax.Precision.HIGHEST)
        doc_length = jnp.dot(
            onehot, lengths[m].astype(jnp.float32), precision=lax.Precision.HIGHEST
        )
        seeds.append((picked / doc_length[:, None]).astype(jnp.bfloat16))

    received = jnp.zeros((tok_rows, feat_width), jnp.bfloat16)
    grad_stream = jnp.zeros((slots, tok_rows, feat_width), jnp.bfloat16)
    kv_total = jnp.zeros((slots, tok_rows, 2 * kv_width), jnp.float32)
    kv_sent = jnp.zeros((slots, wide_rows - tok_rows, 2 * kv_width), jnp.bfloat16)
    gain_total = jnp.zeros((feat_width,), jnp.float32)
    returned_kv = [jnp.zeros((tok_rows, 2 * kv_width), jnp.float32) for _ in range(micro_count)]
    for time_step in range(time_steps):
        raw_index = time_step - (last_segment - section)
        working_buffer = (raw_index >= 0) & (raw_index < micro_count)
        microbatch_index = jnp.clip(raw_index, 0, micro_count - 1)
        slot = jnp.where(working_buffer, microbatch_index, micro_count)
        out_grad = jnp.where(
            section == last_segment, pick(seeds, microbatch_index), received
        )
        stream_grad, gain_part, key_grad, value_grad = attn_bwd_at(
            microbatch_index.astype(jnp.int32).reshape(1),
            stream_store,
            gain_row[None],
            out_grad,
            attended_store,
            kv_stack,
            log_store,
            lower_stack,
            upper,
            key_row,
        )
        kv_grad = jnp.concatenate([key_grad, value_grad], axis=-1)
        gain_total = gain_total + jnp.where(working_buffer, gain_part, 0.0)
        grad_stream = lax.dynamic_update_index_in_dim(grad_stream, stream_grad, slot, 0)
        if time_step < time_steps - 1:
            received = shifted(stream_grad, "pipe", -1)
        kv_total = lax.dynamic_update_index_in_dim(
            kv_total, kv_grad[SPAN * tok_rows :], slot, 0
        )
        kv_sent = lax.dynamic_update_index_in_dim(
            kv_sent, kv_grad[: SPAN * tok_rows].astype(jnp.bfloat16), slot, 0
        )
        for m in range(micro_count):
            if time_step == m + segment_count - 1:
                for distance in range(1, SPAN + 1):
                    lo = (SPAN - distance) * tok_rows
                    returned = shifted(kv_sent[m, lo : lo + tok_rows], "ctx", -distance)
                    returned_kv[m] = returned_kv[m] + returned.astype(jnp.float32)

    kv_out = (kv_total[:micro_count] + jnp.stack(returned_kv)).astype(jnp.bfloat16)
    gain_sum = butterfly_sum(gain_total, "ctx")
    return (
        grad_stream[:micro_count][None],
        kv_out[:, :, :kv_width][None],
        kv_out[:, :, kv_width:][None],
        gain_sum.reshape(1, feat_width),
    )


def solution(mesh):
    placed = (
        P(None, "ctx", None),
        P("pipe", None),
        P("pipe", None, "ctx", None),
        P("pipe", None, "ctx", None),
        P(),
        P(),
        P(None, "ctx"),
        P(),
    )
    return jax.shard_map(
        per_device,
        mesh=mesh,
        in_specs=placed,
        out_specs=(
            P("pipe", None, "ctx", None),
            P("pipe", None, "ctx", None),
            P("pipe", None, "ctx", None),
            P("pipe", None),
        ),
        check_vma=False,
    )
```

```python
import functools

import jax
import jax.numpy as jnp
from jax import lax
from jax.experimental import pallas as pl
from jax.experimental.pallas import tpu as pltpu
from jax.sharding import PartitionSpec as P


HEAD_DIM = 128
SPAN = 2


NORM_EPS = 1e-05


def shifted(x, axis, by):
    size = lax.axis_size(axis)
    pairs = [(i, i + by) for i in range(size) if 0 <= i + by < size]
    return lax.ppermute(x, axis, pairs)


def butterfly_sum(x, axis):
    size = lax.axis_size(axis)
    radices = []
    rest = size
    while rest % 4 == 0:
        radices.append(4)
        rest //= 4
    while rest % 2 == 0:
        radices.append(2)
        rest //= 2
    if rest != 1:
        return lax.psum(x, axis)
    me = lax.axis_index(axis)
    stride = 1
    for radix in radices:
        digit = (me // stride) % radix
        got = [x]
        for offset in range(1, radix):
            pairs = []
            for i in range(size):
                d = (i // stride) % radix
                pairs.append((i, i + (((d - offset) % radix) - d) * stride))
            got.append(lax.ppermute(x, axis, pairs))
        placed = []
        for a in range(radix):
            pick_a = got[0]
            for offset in range(1, radix):
                pick_a = jnp.where((a - digit) % radix == offset, got[offset], pick_a)
            placed.append(pick_a)
        while len(placed) > 1:
            placed = [placed[i] + placed[i + 1] for i in range(0, len(placed), 2)]
        x = placed[0]
        stride *= radix
    return x


NT = (((1,), (1,)), ((), ()))
TN = (((0,), (0,)), ((), ()))


def norm_in_kernel(stream_ref, gain_ref):
    values_f = stream_ref[...].astype(jnp.float32)
    inv_rms = lax.rsqrt(jnp.mean(values_f * values_f, axis=1, keepdims=True) + NORM_EPS)
    normed = values_f * inv_rms
    return values_f, inv_rms, normed, (normed * gain_ref[...]).astype(jnp.bfloat16)


def fwd_kernel(x_ref, gain_ref, k_ref, v_ref, lo_ref, hi_ref, kp_ref, out_ref, o_ref, lt_ref, *, heads, share, scale):
    values_f, _, _, queries = norm_in_kernel(x_ref, gain_ref)
    rows = x_ref.shape[0]
    kpos = kp_ref[...]
    allowed = ((kpos >= lo_ref[...]) & (kpos <= hi_ref[...]))[None]
    for g in range(heads // share):
        gs = slice(g * HEAD_DIM, (g + 1) * HEAD_DIM)
        members = range(g * share, (g + 1) * share)
        q = jnp.concatenate([queries[:, h * HEAD_DIM : (h + 1) * HEAD_DIM] for h in members], axis=0)
        s = lax.dot_general(q, k_ref[:, gs], NT, preferred_element_type=jnp.float32) * scale
        s = s.reshape(share, rows, s.shape[-1])
        tot = jnp.sum(jnp.where(allowed, jnp.exp(s), 0.0), axis=2, keepdims=True)
        lt = jnp.log(tot)
        w = jnp.where(allowed, jnp.exp(s - lt), 0.0).astype(jnp.bfloat16)
        o = jnp.dot(w.reshape(share * rows, -1), v_ref[:, gs], preferred_element_type=jnp.float32)
        for j, h in enumerate(members):
            hs = slice(h * HEAD_DIM, (h + 1) * HEAD_DIM)
            att = o[j * rows : (j + 1) * rows].astype(jnp.bfloat16)
            o_ref[:, hs] = att
            out_ref[:, hs] = (values_f[:, hs] + att.astype(jnp.float32)).astype(out_ref.dtype)
            lt_ref[:, h : h + 1] = lt[j]


def bwd_kernel(x_ref, gain_ref, do_ref, att_ref, k_ref, v_ref, lt_ref, lo_ref, hi_ref, kp_ref, *outs, heads, share, scale, part):
    if part == 0:
        sg_ref, gp_ref, dq_ref = outs
    else:
        dk_ref, dv_ref = outs
    _, inv_rms, normed, queries = norm_in_kernel(x_ref, gain_ref)
    rows = x_ref.shape[0]
    kpos = kp_ref[...]
    allowed = ((kpos >= lo_ref[...]) & (kpos <= hi_ref[...]))[None]
    for g in range(heads // share):
        gs = slice(g * HEAD_DIM, (g + 1) * HEAD_DIM)
        members = range(g * share, (g + 1) * share)
        cols = [slice(h * HEAD_DIM, (h + 1) * HEAD_DIM) for h in members]
        q = jnp.concatenate([queries[:, c] for c in cols], axis=0)
        do = jnp.concatenate([do_ref[:, c] for c in cols], axis=0)
        att = jnp.concatenate([att_ref[:, c] for c in cols], axis=0)
        lt = jnp.stack([lt_ref[:, h : h + 1] for h in members])
        k = k_ref[:, gs]
        v = v_ref[:, gs]
        od = jnp.sum(do.astype(jnp.float32) * att.astype(jnp.float32), axis=1, keepdims=True)
        s = lax.dot_general(q, k, NT, preferred_element_type=jnp.float32) * scale
        s = s.reshape(share, rows, s.shape[-1])
        p = jnp.where(allowed, jnp.exp(s - lt), 0.0).reshape(share * rows, -1)
        dp = lax.dot_general(do, v, NT, preferred_element_type=jnp.float32)
        ds = (p * (dp - od) * scale).astype(jnp.bfloat16)
        w = p.astype(jnp.bfloat16)
        if part == 0:
            dq = jnp.dot(ds, k, preferred_element_type=jnp.float32)
            for j, c in enumerate(cols):
                dq_ref[:, c] = dq[j * rows : (j + 1) * rows]
        else:
            dk_ref[:, gs] = lax.dot_general(ds, q, TN, preferred_element_type=jnp.float32)
            dv_ref[:, gs] = lax.dot_general(w, do, TN, preferred_element_type=jnp.float32)
    if part != 0:
        return
    query_grad = dq_ref[...]
    gp_ref[...] = jnp.sum(query_grad * normed, axis=0, keepdims=True)
    normed_grad = query_grad * gain_ref[...]
    norm_grad = inv_rms * (
        normed_grad - normed * jnp.mean(normed_grad * normed, axis=1, keepdims=True)
    )
    sg_ref[...] = (do_ref[...].astype(jnp.float32) + norm_grad).astype(sg_ref.dtype)


def attn_fwd(x, gain, k, v, lo, hi, kp):
    rows, width = x.shape
    heads = width // HEAD_DIM
    share = heads // (k.shape[1] // HEAD_DIM)
    kern = functools.partial(fwd_kernel, heads=heads, share=share, scale=HEAD_DIM ** -0.5)
    return pl.pallas_call(
        kern,
        out_shape=(
            jax.ShapeDtypeStruct((rows, width), jnp.bfloat16),
            jax.ShapeDtypeStruct((rows, width), jnp.bfloat16),
            jax.ShapeDtypeStruct((rows, heads), jnp.float32),
        ),
    )(x, gain, k, v, lo, hi, kp)


def attn_bwd(x, gain, do, att, k, v, lt, lo, hi, kp):
    rows, width = x.shape
    heads = width // HEAD_DIM
    share = heads // (k.shape[1] // HEAD_DIM)
    kern = functools.partial(bwd_kernel, heads=heads, share=share, scale=HEAD_DIM ** -0.5)
    operands = (x, gain, do, att, k, v, lt, lo, hi, kp)
    sg, gp = pl.pallas_call(
        functools.partial(kern, part=0),
        out_shape=(
            jax.ShapeDtypeStruct((rows, width), jnp.bfloat16),
            jax.ShapeDtypeStruct((1, width), jnp.float32),
        ),
        scratch_shapes=[pltpu.VMEM((rows, width), jnp.float32)],
    )(*operands)
    dk, dv = pl.pallas_call(
        functools.partial(kern, part=1),
        out_shape=(
            jax.ShapeDtypeStruct(k.shape, jnp.float32),
            jax.ShapeDtypeStruct(v.shape, jnp.float32),
        ),
    )(*operands)
    return sg, gp[0], dk, dv


def per_device(hidden, gain, keys, values, cotangent, lengths, doc_start, block_mask):
    section = lax.axis_index("pipe")
    segment_count = lax.axis_size("pipe")
    index_of_block = lax.axis_index("ctx")
    micro_count, tok_rows, feat_width = hidden.shape
    kv_width = keys.shape[3]
    groups = kv_width // HEAD_DIM
    group_share = feat_width // HEAD_DIM // groups
    gain_row = gain[0]
    last_segment = segment_count - 1
    offsets = jnp.arange(tok_rows, dtype=jnp.int32)
    own_pos = index_of_block * tok_rows + offsets
    wide_rows = (SPAN + 1) * tok_rows
    key_pos = (index_of_block - SPAN) * tok_rows + jnp.arange(wide_rows, dtype=jnp.int32)
    time_steps = micro_count + segment_count - 1

    kv_own = jnp.concatenate([keys[0], values[0]], axis=-1)

    def window_of(own):
        return jnp.concatenate(
            [shifted(own, "ctx", distance) for distance in range(SPAN, 0, -1)] + [own]
        )

    kv_wide = [window_of(kv_own[0])] + [None] * (micro_count - 1)
    lower_all = [doc_start[m][:, None] for m in range(micro_count)]
    upper = own_pos[:, None]
    key_row = key_pos[None, :]

    def pick(items, index):
        out = items[0]
        for m in range(1, len(items)):
            out = jnp.where(index == m, items[m], out)
        return out

    slots = micro_count + 1
    received = jnp.zeros((tok_rows, feat_width), jnp.bfloat16)
    stream_store = jnp.zeros((slots, tok_rows, feat_width), jnp.bfloat16)
    attended_store = jnp.zeros((slots, tok_rows, feat_width), jnp.bfloat16)
    log_store = jnp.zeros((slots, tok_rows, groups * group_share), jnp.float32)
    for time_step in range(time_steps):
        raw_index = time_step - section
        working_buffer = (raw_index >= 0) & (raw_index < micro_count)
        microbatch_index = jnp.clip(raw_index, 0, micro_count - 1)
        slot = jnp.where(working_buffer, microbatch_index, micro_count)
        ready = [m for m in range(micro_count) if kv_wide[m] is not None]
        window = pick([kv_wide[m] for m in ready], jnp.minimum(microbatch_index, len(ready) - 1))
        stream_in = jnp.where(section == 0, hidden[microbatch_index], received)
        stream_out, attended, log_total = attn_fwd(
            stream_in,
            gain_row[None],
            window[:, :kv_width],
            window[:, kv_width:],
            pick(lower_all, microbatch_index),
            upper,
            key_row,
        )
        for m in range(micro_count):
            if kv_wide[m] is None and m == time_step + 1:
                tied, _ = lax.optimization_barrier((kv_own[m], attended))
                kv_wide[m] = window_of(tied)
        stream_store = lax.dynamic_update_index_in_dim(stream_store, stream_in, slot, 0)
        attended_store = lax.dynamic_update_index_in_dim(attended_store, attended, slot, 0)
        log_store = lax.dynamic_update_index_in_dim(log_store, log_total, slot, 0)
        if time_step < time_steps - 1:
            received = shifted(stream_out, "pipe", 1)
    key_wide = [kv_wide[m][:, :kv_width] for m in range(micro_count)]
    value_wide = [kv_wide[m][:, kv_width:] for m in range(micro_count)]

    doc_ends = jnp.cumsum(lengths, axis=1)
    doc_starts = doc_ends - lengths
    seeds = []
    for m in range(micro_count):
        onehot = (
            (own_pos[:, None] >= doc_starts[m][None, :]) & (own_pos[:, None] < doc_ends[m][None, :])
        ).astype(jnp.float32)
        picked = jnp.dot(onehot, cotangent[m], precision=lax.Precision.HIGHEST)
        doc_length = jnp.dot(
            onehot, lengths[m].astype(jnp.float32), precision=lax.Precision.HIGHEST
        )
        seeds.append((picked / doc_length[:, None]).astype(jnp.bfloat16))

    received = jnp.zeros((tok_rows, feat_width), jnp.bfloat16)
    grad_stream = jnp.zeros((slots, tok_rows, feat_width), jnp.bfloat16)
    kv_total = jnp.zeros((slots, tok_rows, 2 * kv_width), jnp.float32)
    kv_sent = jnp.zeros((slots, wide_rows - tok_rows, 2 * kv_width), jnp.bfloat16)
    gain_total = jnp.zeros((feat_width,), jnp.float32)
    returned_kv = [jnp.zeros((tok_rows, 2 * kv_width), jnp.float32) for _ in range(micro_count)]
    for time_step in range(time_steps):
      raw_index = time_step - (last_segment - section)
      working_buffer = (raw_index >= 0) & (raw_index < micro_count)
      microbatch_index = jnp.clip(raw_index, 0, micro_count - 1)
      slot = jnp.where(working_buffer, microbatch_index, micro_count)
      out_grad = jnp.where(
          section == last_segment, pick(seeds, microbatch_index), received
      )
      stream_grad, gain_part, key_grad, value_grad = attn_bwd(
          lax.dynamic_index_in_dim(stream_store, microbatch_index, 0, keepdims=False),
          gain_row[None],
          out_grad,
          lax.dynamic_index_in_dim(attended_store, microbatch_index, 0, keepdims=False),
          pick(key_wide, microbatch_index),
          pick(value_wide, microbatch_index),
          lax.dynamic_index_in_dim(log_store, microbatch_index, 0, keepdims=False),
          pick(lower_all, microbatch_index),
          upper,
          key_row,
      )
      kv_grad = jnp.concatenate([key_grad, value_grad], axis=-1)
      gain_total = gain_total + jnp.where(working_buffer, gain_part, 0.0)
      grad_stream = lax.dynamic_update_index_in_dim(grad_stream, stream_grad, slot, 0)
      if time_step < time_steps - 1:
          received = shifted(stream_grad, "pipe", -1)
      kv_total = lax.dynamic_update_index_in_dim(
          kv_total, kv_grad[SPAN * tok_rows :], slot, 0
      )
      kv_sent = lax.dynamic_update_index_in_dim(
          kv_sent, kv_grad[: SPAN * tok_rows].astype(jnp.bfloat16), slot, 0
      )
      for m in range(micro_count):
          if time_step == m + segment_count - 1:
              for distance in range(1, SPAN + 1):
                  lo = (SPAN - distance) * tok_rows
                  returned = shifted(kv_sent[m, lo : lo + tok_rows], "ctx", -distance)
                  returned_kv[m] = returned_kv[m] + returned.astype(jnp.float32)

    kv_out = (kv_total[:micro_count] + jnp.stack(returned_kv)).astype(jnp.bfloat16)
    gain_sum = butterfly_sum(gain_total, "ctx")
    return (
        grad_stream[:micro_count][None],
        kv_out[:, :, :kv_width][None],
        kv_out[:, :, kv_width:][None],
        gain_sum.reshape(1, feat_width),
    )


def solution(mesh):
    placed = (
        P(None, "ctx", None),
        P("pipe", None),
        P("pipe", None, "ctx", None),
        P("pipe", None, "ctx", None),
        P(),
        P(),
        P(None, "ctx"),
        P(),
    )
    return jax.shard_map(
        per_device,
        mesh=mesh,
        in_specs=placed,
        out_specs=(
            P("pipe", None, "ctx", None),
            P("pipe", None, "ctx", None),
            P("pipe", None, "ctx", None),
            P("pipe", None),
        ),
        check_vma=False,
    )
```

```python
import functools

import jax
import jax.numpy as jnp
from jax import lax
from jax.experimental import pallas as pl
from jax.experimental.pallas import tpu as pltpu
from jax.sharding import PartitionSpec as P

HEAD_DIM = 128
SPAN = 2
CHUNKS = 1


NORM_EPS = 1e-05


def shifted(x, axis, by):
    size = lax.axis_size(axis)
    pairs = [(i, i + by) for i in range(size) if 0 <= i + by < size]
    return lax.ppermute(x, axis, pairs)


def butterfly_sum(x, axis):
    size = lax.axis_size(axis)
    radices = []
    rest = size
    while rest % 4 == 0:
        radices.append(4)
        rest //= 4
    while rest % 2 == 0:
        radices.append(2)
        rest //= 2
    if rest != 1:
        return lax.psum(x, axis)
    me = lax.axis_index(axis)
    stride = 1
    for radix in radices:
        digit = (me // stride) % radix
        got = [x]
        for offset in range(1, radix):
            pairs = []
            for i in range(size):
                d = (i // stride) % radix
                pairs.append((i, i + (((d - offset) % radix) - d) * stride))
            got.append(lax.ppermute(x, axis, pairs))
        placed = []
        for a in range(radix):
            pick_a = got[0]
            for offset in range(1, radix):
                pick_a = jnp.where((a - digit) % radix == offset, got[offset], pick_a)
            placed.append(pick_a)
        while len(placed) > 1:
            placed = [placed[i] + placed[i + 1] for i in range(0, len(placed), 2)]
        x = placed[0]
        stride *= radix
    return x


NT = (((1,), (1,)), ((), ()))
TN = (((0,), (0,)), ((), ()))

def norm_in_kernel(stream_ref, gain_ref):
    values_f = stream_ref[...].astype(jnp.float32)
    inv_rms = lax.rsqrt(jnp.mean(values_f * values_f, axis=1, keepdims=True) + NORM_EPS)
    normed = values_f * inv_rms
    return values_f, inv_rms, normed, (normed * gain_ref[...]).astype(jnp.bfloat16)


def fwd_kernel(x_ref, gain_ref, k_ref, v_ref, lo_ref, hi_ref, kp_ref, out_ref, o_ref, lt_ref, *, heads, share, scale):
    values_f, _, _, queries = norm_in_kernel(x_ref, gain_ref)
    rows = x_ref.shape[0]
    kpos = kp_ref[...]
    allowed = ((kpos >= lo_ref[...]) & (kpos <= hi_ref[...]))[None]
    for g in range(heads // share):
        gs = slice(g * HEAD_DIM, (g + 1) * HEAD_DIM)
        members = range(g * share, (g + 1) * share)
        q = jnp.concatenate([queries[:, h * HEAD_DIM : (h + 1) * HEAD_DIM] for h in members], axis=0)
        s = lax.dot_general(q, k_ref[:, gs], NT, preferred_element_type=jnp.float32) * scale
        s = s.reshape(share, rows, s.shape[-1])
        tot = jnp.sum(jnp.where(allowed, jnp.exp(s), 0.0), axis=2, keepdims=True)
        lt = jnp.log(tot)
        w = jnp.where(allowed, jnp.exp(s - lt), 0.0).astype(jnp.bfloat16)
        o = jnp.dot(w.reshape(share * rows, -1), v_ref[:, gs], preferred_element_type=jnp.float32)
        for j, h in enumerate(members):
            hs = slice(h * HEAD_DIM, (h + 1) * HEAD_DIM)
            att = o[j * rows : (j + 1) * rows].astype(jnp.bfloat16)
            o_ref[:, hs] = att
            out_ref[:, hs] = (values_f[:, hs] + att.astype(jnp.float32)).astype(out_ref.dtype)
            lt_ref[:, h : h + 1] = lt[j]


def bwd_kernel(x_ref, gain_ref, do_ref, att_ref, k_ref, v_ref, lt_ref, lo_ref, hi_ref, kp_ref, sg_ref, gp_ref, dk_ref, dv_ref, dq_ref, *, heads, share, scale):
    _, inv_rms, normed, queries = norm_in_kernel(x_ref, gain_ref)
    rows = x_ref.shape[0]
    kpos = kp_ref[...]
    allowed = ((kpos >= lo_ref[...]) & (kpos <= hi_ref[...]))[None]
    for g in range(heads // share):
        gs = slice(g * HEAD_DIM, (g + 1) * HEAD_DIM)
        members = range(g * share, (g + 1) * share)
        cols = [slice(h * HEAD_DIM, (h + 1) * HEAD_DIM) for h in members]
        q = jnp.concatenate([queries[:, c] for c in cols], axis=0)
        do = jnp.concatenate([do_ref[:, c] for c in cols], axis=0)
        att = jnp.concatenate([att_ref[:, c] for c in cols], axis=0)
        lt = jnp.stack([lt_ref[:, h : h + 1] for h in members])
        k = k_ref[:, gs]
        v = v_ref[:, gs]
        od = jnp.sum(do.astype(jnp.float32) * att.astype(jnp.float32), axis=1, keepdims=True)
        s = lax.dot_general(q, k, NT, preferred_element_type=jnp.float32) * scale
        s = s.reshape(share, rows, s.shape[-1])
        p = jnp.where(allowed, jnp.exp(s - lt), 0.0).reshape(share * rows, -1)
        dp = lax.dot_general(do, v, NT, preferred_element_type=jnp.float32)
        ds = (p * (dp - od) * scale).astype(jnp.bfloat16)
        w = p.astype(jnp.bfloat16)
        dq = jnp.dot(ds, k, preferred_element_type=jnp.float32)
        for j, c in enumerate(cols):
            dq_ref[:, c] = dq[j * rows : (j + 1) * rows]
        dk_ref[:, gs] = lax.dot_general(ds, q, TN, preferred_element_type=jnp.float32)
        dv_ref[:, gs] = lax.dot_general(w, do, TN, preferred_element_type=jnp.float32)
    query_grad = dq_ref[...]
    gp_ref[...] = jnp.sum(query_grad * normed, axis=0, keepdims=True)
    normed_grad = query_grad * gain_ref[...]
    norm_grad = inv_rms * (
        normed_grad - normed * jnp.mean(normed_grad * normed, axis=1, keepdims=True)
    )
    sg_ref[...] = (do_ref[...].astype(jnp.float32) + norm_grad).astype(sg_ref.dtype)


def attn_fwd(x, gain, k, v, lo, hi, kp):
    rows, width = x.shape
    heads = width // HEAD_DIM
    share = heads // (k.shape[1] // HEAD_DIM)
    kern = functools.partial(fwd_kernel, heads=heads, share=share, scale=HEAD_DIM ** -0.5)
    return pl.pallas_call(
        kern,
        out_shape=(
            jax.ShapeDtypeStruct((rows, width), jnp.bfloat16),
            jax.ShapeDtypeStruct((rows, width), jnp.bfloat16),
            jax.ShapeDtypeStruct((rows, heads), jnp.float32),
        ),
    )(x, gain, k, v, lo, hi, kp)


def attn_bwd(x, gain, do, att, k, v, lt, lo, hi, kp):
    rows, width = x.shape
    heads = width // HEAD_DIM
    share = heads // (k.shape[1] // HEAD_DIM)
    kern = functools.partial(bwd_kernel, heads=heads, share=share, scale=HEAD_DIM ** -0.5)
    sg, gp, dk, dv = pl.pallas_call(
        kern,
        out_shape=(
            jax.ShapeDtypeStruct((rows, width), jnp.bfloat16),
            jax.ShapeDtypeStruct((1, width), jnp.float32),
            jax.ShapeDtypeStruct(k.shape, jnp.float32),
            jax.ShapeDtypeStruct(v.shape, jnp.float32),
        ),
        scratch_shapes=[pltpu.VMEM((rows, width), jnp.float32)],
    )(x, gain, do, att, k, v, lt, lo, hi, kp)
    return sg, gp[0], dk, dv


def per_device(hidden, gain, keys, values, cotangent, lengths, doc_start, block_mask):
    section = lax.axis_index("pipe")
    segment_count = lax.axis_size("pipe")
    index_of_block = lax.axis_index("ctx")
    micro_count, tok_rows, feat_width = hidden.shape
    kv_width = keys.shape[3]
    groups = kv_width // HEAD_DIM
    group_share = feat_width // HEAD_DIM // groups
    gain_row = gain[0]
    last_segment = segment_count - 1
    offsets = jnp.arange(tok_rows, dtype=jnp.int32)
    own_pos = index_of_block * tok_rows + offsets
    wide_rows = (SPAN + 1) * tok_rows
    key_pos = (index_of_block - SPAN) * tok_rows + jnp.arange(wide_rows, dtype=jnp.int32)
    time_steps = micro_count + segment_count - 1

    kv_own = jnp.concatenate([keys[0], values[0]], axis=-1)
    def window_of(own):
        return jnp.concatenate(
            [shifted(own, "ctx", distance) for distance in range(SPAN, 0, -1)] + [own]
        )

    kv_wide = [window_of(kv_own[0])] + [None] * (micro_count - 1)
    lower_all = [doc_start[m][:, None] for m in range(micro_count)]
    upper = own_pos[:, None]
    key_row = key_pos[None, :]

    def pick(items, index):
        out = items[0]
        for m in range(1, len(items)):
            out = jnp.where(index == m, items[m], out)
        return out

    slots = micro_count + 1
    received = jnp.zeros((tok_rows, feat_width), jnp.bfloat16)
    stream_store = jnp.zeros((slots, tok_rows, feat_width), jnp.bfloat16)
    attended_store = jnp.zeros((slots, tok_rows, feat_width), jnp.bfloat16)
    log_store = jnp.zeros((slots, tok_rows, groups * group_share), jnp.float32)
    for time_step in range(time_steps):
        raw_index = time_step - section
        working_buffer = (raw_index >= 0) & (raw_index < micro_count)
        microbatch_index = jnp.clip(raw_index, 0, micro_count - 1)
        slot = jnp.where(working_buffer, microbatch_index, micro_count)
        ready = [m for m in range(micro_count) if kv_wide[m] is not None]
        window = pick([kv_wide[m] for m in ready], jnp.minimum(microbatch_index, len(ready) - 1))
        stream_in = jnp.where(section == 0, hidden[microbatch_index], received)
        stream_out, attended, log_total = attn_fwd(
            stream_in,
            gain_row[None],
            window[:, :kv_width],
            window[:, kv_width:],
            pick(lower_all, microbatch_index),
            upper,
            key_row,
        )
        for m in range(micro_count):
            if kv_wide[m] is None and m == time_step + 1:
                kv_wide[m] = window_of(kv_own[m])
        stream_store = lax.dynamic_update_index_in_dim(stream_store, stream_in, slot, 0)
        attended_store = lax.dynamic_update_index_in_dim(attended_store, attended, slot, 0)
        log_store = lax.dynamic_update_index_in_dim(log_store, log_total, slot, 0)
        if time_step < time_steps - 1:
            received = shifted(stream_out, "pipe", 1)
    key_wide = [kv_wide[m][:, :kv_width] for m in range(micro_count)]
    value_wide = [kv_wide[m][:, kv_width:] for m in range(micro_count)]

    doc_ends = jnp.cumsum(lengths, axis=1)
    doc_starts = doc_ends - lengths
    seeds = []
    for m in range(micro_count):
        onehot = (
            (own_pos[:, None] >= doc_starts[m][None, :]) & (own_pos[:, None] < doc_ends[m][None, :])
        ).astype(jnp.float32)
        picked = jnp.dot(onehot, cotangent[m], precision=lax.Precision.HIGHEST)
        doc_length = jnp.dot(
            onehot, lengths[m].astype(jnp.float32), precision=lax.Precision.HIGHEST
        )
        seeds.append((picked / doc_length[:, None]).astype(jnp.bfloat16))

    received = jnp.zeros((tok_rows, feat_width), jnp.bfloat16)
    grad_stream = jnp.zeros((slots, tok_rows, feat_width), jnp.bfloat16)
    kv_total = jnp.zeros((slots, tok_rows, 2 * kv_width), jnp.float32)
    kv_sent = jnp.zeros((slots, wide_rows - tok_rows, 2 * kv_width), jnp.bfloat16)
    gain_total = jnp.zeros((feat_width,), jnp.float32)
    returned_kv = [jnp.zeros((tok_rows, 2 * kv_width), jnp.float32) for _ in range(micro_count)]
    for time_step in range(time_steps):
        raw_index = time_step - (last_segment - section)
        working_buffer = (raw_index >= 0) & (raw_index < micro_count)
        microbatch_index = jnp.clip(raw_index, 0, micro_count - 1)
        slot = jnp.where(working_buffer, microbatch_index, micro_count)
        out_grad = jnp.where(
            section == last_segment, pick(seeds, microbatch_index), received
        )
        stream_grad, gain_part, key_grad, value_grad = attn_bwd(
            lax.dynamic_index_in_dim(stream_store, microbatch_index, 0, keepdims=False),
            gain_row[None],
            out_grad,
            lax.dynamic_index_in_dim(attended_store, microbatch_index, 0, keepdims=False),
            pick(key_wide, microbatch_index),
            pick(value_wide, microbatch_index),
            lax.dynamic_index_in_dim(log_store, microbatch_index, 0, keepdims=False),
            pick(lower_all, microbatch_index),
            upper,
            key_row,
        )
        kv_grad = jnp.concatenate([key_grad, value_grad], axis=-1)
        gain_total = gain_total + jnp.where(working_buffer, gain_part, 0.0)
        grad_stream = lax.dynamic_update_index_in_dim(grad_stream, stream_grad, slot, 0)
        if time_step < time_steps - 1:
            received = shifted(stream_grad, "pipe", -1)
        kv_total = lax.dynamic_update_index_in_dim(
            kv_total, kv_grad[SPAN * tok_rows :], slot, 0
        )
        kv_sent = lax.dynamic_update_index_in_dim(
            kv_sent, kv_grad[: SPAN * tok_rows].astype(jnp.bfloat16), slot, 0
        )
        for m in range(micro_count):
            if time_step == m + segment_count - 1:
                for distance in range(1, SPAN + 1):
                    lo = (SPAN - distance) * tok_rows
                    returned = shifted(kv_sent[m, lo : lo + tok_rows], "ctx", -distance)
                    returned_kv[m] = returned_kv[m] + returned.astype(jnp.float32)

    kv_out = (kv_total[:micro_count] + jnp.stack(returned_kv)).astype(jnp.bfloat16)
    gain_sum = butterfly_sum(gain_total, "ctx")
    return (
        grad_stream[:micro_count][None],
        kv_out[:, :, :kv_width][None],
        kv_out[:, :, kv_width:][None],
        gain_sum.reshape(1, feat_width),
    )


def solution(mesh):
    placed = (
        P(None, "ctx", None),
        P("pipe", None),
        P("pipe", None, "ctx", None),
        P("pipe", None, "ctx", None),
        P(),
        P(),
        P(None, "ctx"),
        P(),
    )
    return jax.shard_map(
        per_device,
        mesh=mesh,
        in_specs=placed,
        out_specs=(
            P("pipe", None, "ctx", None),
            P("pipe", None, "ctx", None),
            P("pipe", None, "ctx", None),
            P("pipe", None),
        ),
        check_vma=False,
    )
```
